32 devices in a mesh: seq: 16 (over z, y, x), tp: 2 (over core).
Axes of the slice: x: 2, y: 2, z: 4, core: 2. Of those that a mesh axis runs over, the one named last changes fastest.
Arguments:
- prefill_hidden: bfloat16 [2048, 5120], P('seq', 'tp'), may hold values from -14 to 14
- prefill_query_rows: bfloat16 [2048, 5120], P('seq', 'tp'), may hold values from -250 to 250
- prefill_key_value: bfloat16 [2, 2048, 1024], P(None, 'seq', 'tp'), may hold values from -5 to 5
- request_prefix_cache: bfloat16 [2, 16, 768, 1024], P(None, 'seq', None, 'tp'), may hold values from -5 to 5
- prefix_lengths: int32 [16], replicated, may hold values from 0 to 768, as said below
- decode_hidden: bfloat16 [4, 5120], P(None, 'tp'), may hold values from -14 to 14
- decode_query_rows: bfloat16 [4, 5120], P(None, 'tp'), may hold values from -250 to 250
- decode_kv: bfloat16 [2, 4, 1024], P(None, None, 'tp'), may hold values from -5 to 5
- decode_slot_cache: bfloat16 [2, 5, 2048, 1024], P(None, None, 'seq', 'tp'), may hold values from -5 to 5
- cache_lengths: int32 [4], replicated, may hold values from 512 to 2048, as said below
- slot_table: int32 [4], replicated, may hold values from 0 to 4, as said below
- out_weight: bfloat16 [5120, 5120], P('tp', 'seq'), may hold values from -0.078125 to 0.078125
- final_gain: bfloat16 [5120], replicated, may hold values from 0.5 to 1.5
- head_weight: bfloat16 [5120, 152064], P(None, ('seq', 'tp')), may hold values from -4 to 4
Outputs:
- prefill_out: bfloat16 [2048, 5120], P('seq', 'tp')
- decode_out: bfloat16 [4, 5120], P(None, 'tp')
- log_probs: float32 [20, 152064], P(None, ('seq', 'tp'))
The draws below stay inside these ranges and needn't reach their ends.
Inputs may be any that keep to these rules, and one draw needn't show every extreme that they name: `prefix_lengths`: some request has no cached prefix and some has exactly 768 cached tokens. `cache_lengths`: some request has exactly 2048 cached tokens. `slot_table`: distinct slots.
All inputs are finite; a program needn't handle non-finite values.
Results may differ from the reference program's by a relative error of at most 0.0035.
Values may be sent and summed in bfloat16 or wider, within the bound.
No kernel may reach another device: no remote copies, remote signals or barrier semaphores. Data moves between devices by JAX's collectives and lax.ppermute only.
A program may use at most 128 MiB of HBM per device.

```python
import math
import jax
import jax.numpy as jnp
from jax import lax

D = 5120
QUERY_HEADS = 40
KEY_HEADS = 8
HEAD_SIZE = 128
VOCAB = 152064
REQUEST_TOKENS = 128
PREFIX_POSITIONS = 768
DECODE_REQUESTS = 4
PREFILL_REQUESTS = 16
CACHE_SLOTS = 5
SLOT_POSITIONS = 2048
PREFILL_TOKENS = 2048


def bounded_gaussian(key, shape):
    return jax.random.truncated_normal(key, -4.0, 4.0, shape, jnp.float32)


def hidden_rows(key, entry_count):
    return bounded_gaussian(jax.random.fold_in(key, 1), (entry_count, D))


def repeat_heads(key_matrix, entry_count):
    deviation_scale = key_matrix.reshape(entry_count, KEY_HEADS, 1, HEAD_SIZE)
    return jnp.broadcast_to(deviation_scale, (entry_count, KEY_HEADS, QUERY_HEADS // KEY_HEADS, HEAD_SIZE)).reshape(entry_count, QUERY_HEADS * HEAD_SIZE)


def prefill_pair(key):
    random_seed_key = jax.random.fold_in(key, 700)
    sampled_values = bounded_gaussian(jax.random.fold_in(random_seed_key, 1), (2, PREFILL_TOKENS, KEY_HEADS * HEAD_SIZE))
    key_matrix = sampled_values[0]
    noise = bounded_gaussian(jax.random.fold_in(random_seed_key, 5), (PREFILL_TOKENS, QUERY_HEADS * HEAD_SIZE))
    query_matrix = noise
    return (jnp.stack([key_matrix, sampled_values[1]]), query_matrix)


def decode_set(key):
    random_seed_key = jax.random.fold_in(key, 800)
    sampled_values = bounded_gaussian(jax.random.fold_in(random_seed_key, 1), (2, DECODE_REQUESTS, KEY_HEADS * HEAD_SIZE))
    strength = jnp.full((DECODE_REQUESTS,), 0.5, jnp.float32)
    noise = bounded_gaussian(jax.random.fold_in(random_seed_key, 4), (DECODE_REQUESTS, QUERY_HEADS * HEAD_SIZE))
    query_matrix = noise + strength[:, None] * repeat_heads(sampled_values[0], DECODE_REQUESTS)
    return (sampled_values, query_matrix)


def slot_draw(key):
    random_seed_key = jax.random.fold_in(key, 300)
    order = jax.random.permutation(jax.random.fold_in(random_seed_key, 1), CACHE_SLOTS - 1)[:DECODE_REQUESTS - 1]
    table = jnp.concatenate([order.astype(jnp.int32), jnp.full((1,), CACHE_SLOTS - 1, jnp.int32)])
    return jax.random.permutation(jax.random.fold_in(random_seed_key, 2), table).astype(jnp.int32)


def draw_prefill_hidden(key, part):
    return hidden_rows(jax.random.fold_in(key, 601), PREFILL_TOKENS).astype(jnp.bfloat16)


def draw_decode_hidden(key, part):
    return hidden_rows(jax.random.fold_in(key, 602), DECODE_REQUESTS).astype(jnp.bfloat16)


def draw_prefill_query_rows(key, part):
    return prefill_pair(key)[1].astype(jnp.bfloat16)


def draw_prefill_key_value(key, part):
    return prefill_pair(key)[0].astype(jnp.bfloat16)


def draw_decode_query_rows(key, part):
    return decode_set(key)[1].astype(jnp.bfloat16)


def draw_decode_kv(key, part):
    return decode_set(key)[0].astype(jnp.bfloat16)


def draw_decode_slot_cache(key, part):
    slot_storage = bounded_gaussian(jax.random.fold_in(key, 900), (2, CACHE_SLOTS, SLOT_POSITIONS, KEY_HEADS * HEAD_SIZE))
    return slot_storage.astype(jnp.bfloat16)


def draw_slot_table(key, part):
    return slot_draw(key)


def draw_cache_lengths(key, part):
    random_seed_key = jax.random.fold_in(key, 400)
    sampled_values = jax.random.randint(jax.random.fold_in(random_seed_key, 1), (DECODE_REQUESTS,), SLOT_POSITIONS // 4, SLOT_POSITIONS + 1)
    chosen = jax.random.randint(jax.random.fold_in(random_seed_key, 2), (), 0, DECODE_REQUESTS)
    return jnp.where(jnp.arange(DECODE_REQUESTS) == chosen, SLOT_POSITIONS, sampled_values).astype(jnp.int32)


def draw_prefix_lengths(key, part):
    random_seed_key = jax.random.fold_in(key, 450)
    sampled_values = jax.random.randint(jax.random.fold_in(random_seed_key, 1), (PREFILL_REQUESTS,), 0, PREFIX_POSITIONS + 1)
    longest = jax.random.randint(jax.random.fold_in(random_seed_key, 2), (), 0, PREFILL_REQUESTS)
    empty_one = (longest + 1 + jax.random.randint(jax.random.fold_in(random_seed_key, 3), (), 0, PREFILL_REQUESTS - 1)) % PREFILL_REQUESTS
    place = jnp.arange(PREFILL_REQUESTS)
    sampled_values = jnp.where(place == longest, PREFIX_POSITIONS, sampled_values)
    return jnp.where(place == empty_one, 0, sampled_values).astype(jnp.int32)


def draw_head_weight(key, part):
    random_seed_key = jax.random.fold_in(key, 1000)
    column_place = jnp.arange(VOCAB).astype(jnp.float32) / VOCAB
    column_scale = 0.5 + 2.5 * column_place
    return (bounded_gaussian(jax.random.fold_in(random_seed_key, 1), (D, VOCAB)) / D ** 0.5 * column_scale[None, :]).astype(jnp.bfloat16)


def steps_of(stream_key, extent, cuts, smallest, high):
    level, own = 1.0, jax.random.fold_in(stream_key, 6)
    for position, parts in cuts:
        heights = jnp.exp(jax.random.uniform(jax.random.fold_in(own, position), (parts,), jnp.float32, smallest / len(cuts), high / len(cuts)))
        level = level * jnp.repeat(heights, extent[position] // parts).reshape([-1 if axis == position else 1 for axis in range(len(extent))])
    return level


def gaussian(rng, dims, scale, reach, shards=(), kind=jnp.bfloat16):
    level = steps_of(rng, dims, shards, -0.22, 0.18) if shards else 1.0
    values = jax.random.normal(rng, dims, jnp.float32) * scale * level
    return jnp.minimum(jnp.maximum(values, -reach), reach).astype(kind)


def setup_inputs(seed: int = 0) -> dict:
    streams_of = jax.random.split(jax.random.key(seed), 15)
    prefill_hidden = draw_prefill_hidden(jax.random.fold_in(streams_of[14], 71), 0)
    prefill_query_rows = draw_prefill_query_rows(jax.random.fold_in(streams_of[14], 71), 0)
    prefill_key_value = draw_prefill_key_value(jax.random.fold_in(streams_of[14], 71), 0)
    request_prefix_cache = gaussian(streams_of[3], (2, PREFILL_REQUESTS, PREFIX_POSITIONS, KEY_HEADS * HEAD_SIZE), 1.0, 5.0, ((1, 16), (3, 2)))
    prefix_lengths = draw_prefix_lengths(jax.random.fold_in(streams_of[14], 71), 0)
    decode_hidden = draw_decode_hidden(jax.random.fold_in(streams_of[14], 71), 0)
    decode_query_rows = draw_decode_query_rows(jax.random.fold_in(streams_of[14], 71), 0)
    decode_kv = draw_decode_kv(jax.random.fold_in(streams_of[14], 71), 0)
    decode_slot_cache = draw_decode_slot_cache(jax.random.fold_in(streams_of[14], 71), 0)
    cache_lengths = draw_cache_lengths(jax.random.fold_in(streams_of[14], 71), 0)
    slot_table = draw_slot_table(jax.random.fold_in(streams_of[14], 71), 0)
    out_weight = gaussian(streams_of[11], (QUERY_HEADS * HEAD_SIZE, D), (QUERY_HEADS * HEAD_SIZE) ** -0.5, 0.078125, ((0, 2), (1, 16)))
    final_gain = jnp.clip(1.0 + 0.1 * jax.random.normal(streams_of[12], (D,), jnp.float32), 0.5, 1.5).astype(jnp.bfloat16)
    head_weight = draw_head_weight(jax.random.fold_in(streams_of[14], 71), 0)
    return {"prefill_hidden": prefill_hidden, "prefill_query_rows": prefill_query_rows, "prefill_key_value": prefill_key_value, "request_prefix_cache": request_prefix_cache, "prefix_lengths": prefix_lengths, "decode_hidden": decode_hidden, "decode_query_rows": decode_query_rows, "decode_kv": decode_kv, "decode_slot_cache": decode_slot_cache, "cache_lengths": cache_lengths, "slot_table": slot_table, "out_weight": out_weight, "final_gain": final_gain, "head_weight": head_weight}


neg_large = -1e+30
exact = lax.Precision.HIGHEST
norm_eps = 1e-06

def reference(prefill_hidden, prefill_query_rows, prefill_key_value, request_prefix_cache, prefix_lengths, decode_hidden, decode_query_rows, decode_kv, decode_slot_cache, cache_lengths, slot_table, out_weight, final_gain, head_weight):
    query_group_width = QUERY_HEADS // KEY_HEADS
    score_scale = 1.0 / math.sqrt(HEAD_SIZE)
    query_matrix = prefill_query_rows.reshape(PREFILL_REQUESTS, REQUEST_TOKENS, KEY_HEADS, query_group_width, HEAD_SIZE)
    request_key_value = jnp.transpose(prefill_key_value.reshape(2, PREFILL_REQUESTS, REQUEST_TOKENS, KEY_HEADS * HEAD_SIZE), (1, 0, 2, 3))
    prefix_all = jnp.transpose(request_prefix_cache, (1, 0, 2, 3))

    def prefill_one(inputs):
        query_rows, prefix_token_rows, current_rows, prefix_end = inputs
        joined_keys = jnp.concatenate([prefix_token_rows[0], current_rows[0]], 0).reshape(PREFIX_POSITIONS + REQUEST_TOKENS, KEY_HEADS, HEAD_SIZE).astype(jnp.float32)
        value_matrix = jnp.concatenate([prefix_token_rows[1], current_rows[1]], 0).reshape(PREFIX_POSITIONS + REQUEST_TOKENS, KEY_HEADS, HEAD_SIZE).astype(jnp.float32)
        key_place = jnp.arange(PREFIX_POSITIONS + REQUEST_TOKENS)
        query_place = jnp.arange(REQUEST_TOKENS)
        live_mask = jnp.where(key_place[None, :] < PREFIX_POSITIONS, key_place[None, :] < prefix_end, key_place[None, :] - PREFIX_POSITIONS <= query_place[:, None])
        scores = jnp.einsum('rkgh,skh->kgrs', query_rows.astype(jnp.float32), joined_keys, precision=exact) * score_scale
        masked = jnp.where(live_mask, scores, neg_large)
        row_max = lax.optimization_barrier(jnp.max(masked, axis=-1, keepdims=True))
        weights = jnp.where(live_mask, jnp.exp(masked - row_max), 0.0)
        row_sum = lax.optimization_barrier(jnp.sum(weights, axis=-1))
        weights_low = weights.astype(jnp.bfloat16).astype(jnp.float32)
        mixed = jnp.einsum('kgrs,skh->rkgh', weights_low, value_matrix, precision=exact)
        result = mixed / jnp.transpose(row_sum, (2, 0, 1))[..., None]
        return result.astype(jnp.bfloat16).reshape(REQUEST_TOKENS, QUERY_HEADS * HEAD_SIZE)
    prefill_attention = lax.map(prefill_one, (query_matrix, prefix_all, request_key_value, prefix_lengths)).reshape(PREFILL_TOKENS, QUERY_HEADS * HEAD_SIZE)
    decode_token_rows = decode_query_rows.reshape(DECODE_REQUESTS, KEY_HEADS, query_group_width, HEAD_SIZE)
    fresh_all = jnp.transpose(decode_kv, (1, 0, 2))

    def decode_one(inputs):
        query_rows, cache_slot_index, cache_len, current_rows = inputs
        joined_keys = jnp.concatenate([decode_slot_cache[0, cache_slot_index], current_rows[0][None]], 0).reshape(SLOT_POSITIONS + 1, KEY_HEADS, HEAD_SIZE).astype(jnp.float32)
        value_matrix = jnp.concatenate([decode_slot_cache[1, cache_slot_index], current_rows[1][None]], 0).reshape(SLOT_POSITIONS + 1, KEY_HEADS, HEAD_SIZE).astype(jnp.float32)
        key_place = jnp.arange(SLOT_POSITIONS + 1)
        live_mask = (key_place < cache_len) | (key_place == SLOT_POSITIONS)
        scores = jnp.einsum('kgh,skh->kgs', query_rows.astype(jnp.float32), joined_keys, precision=exact) * score_scale
        masked = jnp.where(live_mask, scores, neg_large)
        row_max = lax.optimization_barrier(jnp.max(masked, axis=-1, keepdims=True))
        weights = jnp.where(live_mask, jnp.exp(masked - row_max), 0.0)
        row_sum = lax.optimization_barrier(jnp.sum(weights, axis=-1))
        mixed = jnp.einsum('kgs,skh->kgh', weights, value_matrix, precision=exact)
        return (mixed / row_sum[..., None]).astype(jnp.bfloat16).reshape(QUERY_HEADS * HEAD_SIZE)
    decode_attention = lax.map(decode_one, (decode_token_rows, slot_table, cache_lengths, fresh_all))
    attention_all = jnp.concatenate([prefill_attention, decode_attention], 0)
    projected = jnp.dot(attention_all, out_weight, preferred_element_type=jnp.float32)
    residual = jnp.concatenate([prefill_hidden, decode_hidden], 0).astype(jnp.float32)
    updated = (residual + projected).astype(jnp.bfloat16)
    prefill_out = updated[:PREFILL_TOKENS]
    decode_out = updated[PREFILL_TOKENS:]
    head_input = jnp.concatenate([decode_out, prefill_out[REQUEST_TOKENS - 1::REQUEST_TOKENS]], 0).astype(jnp.float32)
    mean_square = lax.optimization_barrier(jnp.mean(head_input * head_input, axis=-1, keepdims=True))
    normed = (head_input * lax.rsqrt(mean_square + norm_eps) * final_gain.astype(jnp.float32)).astype(jnp.bfloat16)
    logits = jnp.dot(normed, head_weight, preferred_element_type=jnp.float32)
    row_max = lax.optimization_barrier(jnp.max(logits, axis=-1, keepdims=True))
    row_sum = lax.optimization_barrier(jnp.sum(jnp.exp(logits - row_max), axis=-1, keepdims=True))
    log_probs = logits - (row_max + jnp.log(row_sum))
    return (prefill_out, decode_out, log_probs)
```

```python
import math

import jax
import jax.numpy as jnp
from jax import lax
from jax.sharding import PartitionSpec as P

QUERY_HEADS = 40
KEY_HEADS = 8
HEAD_SIZE = 128


neg_large = -1e30
exact = lax.Precision.HIGHEST
norm_eps = 1e-06


def local(
    prefill_hidden,
    prefill_query_rows,
    prefill_key_value,
    request_prefix_cache,
    prefix_lengths,
    decode_hidden,
    decode_query_rows,
    decode_kv,
    decode_slot_cache,
    cache_lengths,
    slot_table,
    out_weight,
    final_gain,
    head_weight,
):
    query_group_width = QUERY_HEADS // KEY_HEADS
    score_scale = 1.0 / math.sqrt(HEAD_SIZE)
    kv_local = prefill_key_value.shape[2] // HEAD_SIZE
    seq_index = lax.axis_index("seq")
    tp_index = lax.axis_index("tp")
    n_seq = lax.axis_size("seq")
    n_tp = lax.axis_size("tp")
    span_len = prefill_query_rows.shape[0]
    prefix_len = request_prefix_cache.shape[2]
    feature_width = prefill_hidden.shape[1]
    model_width = feature_width * n_tp
    column_width = out_weight.shape[1]
    decode_count = decode_query_rows.shape[0]

    ctx_local = decode_slot_cache.shape[2]
    chosen = jnp.take(decode_slot_cache, slot_table, axis=1)
    positions = seq_index * ctx_local + jnp.arange(ctx_local)
    decode_live = (positions[None, :] < cache_lengths[:, None])[:, None, None, :]
    decode_token_rows = decode_query_rows.reshape(
        decode_count, kv_local, query_group_width, HEAD_SIZE
    )
    cache_keys = chosen[0].reshape(decode_count, ctx_local, kv_local, HEAD_SIZE)
    cache_values = chosen[1].reshape(decode_count, ctx_local, kv_local, HEAD_SIZE)
    decode_scores = (
        jnp.einsum(
            "bkgh,bskh->bkgs", decode_token_rows, cache_keys, preferred_element_type=jnp.float32
        )
        * score_scale
    )
    decode_masked = jnp.where(decode_live, decode_scores, neg_large)
    decode_max = jnp.max(decode_masked, axis=-1)
    decode_weights = jnp.where(decode_live, jnp.exp(decode_masked - decode_max[..., None]), 0.0)
    decode_sum = jnp.sum(decode_weights, axis=-1)
    decode_mixed = jnp.einsum(
        "bkgs,bskh->bkgh", decode_weights, cache_values.astype(jnp.float32), precision=exact
    )
    packed = jnp.concatenate([decode_max[..., None], decode_sum[..., None], decode_mixed], -1)
    every_part = lax.all_gather(packed, "seq", axis=0)

    prefix_end = lax.dynamic_slice_in_dim(prefix_lengths, seq_index, 1)[0]
    query_matrix = prefill_query_rows.reshape(span_len, kv_local, query_group_width, HEAD_SIZE)
    joined_keys = jnp.concatenate([request_prefix_cache[0, 0], prefill_key_value[0]], 0).reshape(
        prefix_len + span_len, kv_local, HEAD_SIZE
    )
    value_matrix = jnp.concatenate([request_prefix_cache[1, 0], prefill_key_value[1]], 0).reshape(
        prefix_len + span_len, kv_local, HEAD_SIZE
    )
    key_place = jnp.arange(prefix_len + span_len)
    query_place = jnp.arange(span_len)
    live_mask = jnp.where(
        key_place[None, :] < prefix_len,
        key_place[None, :] < prefix_end,
        key_place[None, :] - prefix_len <= query_place[:, None],
    )
    scores = (
        jnp.einsum("rkgh,skh->kgrs", query_matrix, joined_keys, preferred_element_type=jnp.float32)
        * score_scale
    )
    masked = jnp.where(live_mask, scores, neg_large)
    row_max = jnp.max(masked, axis=-1, keepdims=True)
    weights = jnp.where(live_mask, jnp.exp(masked - row_max), 0.0)
    row_sum = jnp.sum(weights, axis=-1)
    weights_low = weights.astype(jnp.bfloat16)
    mixed = jnp.einsum(
        "kgrs,skh->rkgh", weights_low, value_matrix, preferred_element_type=jnp.float32
    )
    prefill_attention = (
        (mixed / jnp.transpose(row_sum, (2, 0, 1))[..., None])
        .astype(jnp.bfloat16)
        .reshape(span_len, -1)
    )
    every_row = lax.all_gather(prefill_attention, "seq", axis=0, tiled=True)

    part_max = every_part[..., 0]
    part_sum = every_part[..., 1]
    part_mixed = every_part[..., 2:]
    best = jnp.max(part_max, axis=0)
    factors = jnp.exp(part_max - best[None])
    totals = jnp.sum(part_sum * factors, axis=0)
    mixtures = jnp.sum(part_mixed * factors[..., None], axis=0)
    own_keys = decode_kv[0].reshape(decode_count, kv_local, HEAD_SIZE)
    own_values = decode_kv[1].reshape(decode_count, kv_local, HEAD_SIZE).astype(jnp.float32)
    own_scores = (
        jnp.einsum("bkgh,bkh->bkg", decode_token_rows, own_keys, preferred_element_type=jnp.float32)
        * score_scale
    )
    final_max = jnp.maximum(best, own_scores)
    factor_one = jnp.exp(best - final_max)
    factor_two = jnp.exp(own_scores - final_max)
    final_sum = totals * factor_one + factor_two
    final_mixed = mixtures * factor_one[..., None] + own_values[:, :, None, :] * factor_two[..., None]
    decode_attention = (
        (final_mixed / final_sum[..., None]).astype(jnp.bfloat16).reshape(decode_count, -1)
    )

    attention_all = jnp.concatenate([every_row, decode_attention], 0)
    column_block = jnp.dot(attention_all, out_weight, preferred_element_type=jnp.float32)
    prefill_block = column_block[: n_seq * span_len].reshape(n_seq, span_len, column_width)

    head_part = jnp.concatenate(
        [column_block[n_seq * span_len :], prefill_block[:, span_len - 1]], 0
    )
    hidden_piece = jnp.concatenate([prefill_hidden[span_len - 1 :], decode_hidden], 0)
    payload = jnp.concatenate(
        [head_part.reshape(-1), hidden_piece.astype(jnp.float32).reshape(-1)]
    )
    head_all = lax.all_gather(payload, ("seq", "tp"), axis=0).reshape(n_seq, n_tp, -1)
    head_rows_count = decode_count + n_seq
    head_partials = head_all[..., : head_rows_count * column_width].reshape(
        n_seq, n_tp, head_rows_count, column_width
    )
    head_projected = jnp.sum(head_partials, axis=1)
    head_projected = jnp.transpose(head_projected, (1, 0, 2)).reshape(head_rows_count, model_width)
    hidden_all = head_all[..., head_rows_count * column_width :].reshape(
        n_seq, n_tp, 1 + decode_count, feature_width
    )
    prefill_last = hidden_all[:, :, 0].reshape(n_seq, model_width)
    decode_full_hidden = jnp.transpose(hidden_all[0, :, 1:], (1, 0, 2)).reshape(
        decode_count, model_width
    )
    head_hidden = jnp.concatenate([decode_full_hidden, prefill_last], 0)
    head_updated = (head_hidden + head_projected).astype(jnp.bfloat16)
    decode_out = lax.dynamic_slice_in_dim(
        head_updated[:decode_count], tp_index * feature_width, feature_width, axis=1
    )

    rows_part = span_len // n_tp
    summed_rows = lax.psum_scatter(prefill_block, "tp", scatter_dimension=1, tiled=True)
    by_source = lax.all_to_all(summed_rows, "seq", split_axis=0, concat_axis=0, tiled=True)
    own_columns = lax.all_to_all(by_source, "tp", split_axis=0, concat_axis=1, tiled=True)
    projected = jnp.transpose(own_columns, (1, 0, 2)).reshape(span_len, feature_width)
    del rows_part
    prefill_out = (prefill_hidden.astype(jnp.float32) + projected).astype(jnp.bfloat16)

    head_input = head_updated.astype(jnp.float32)
    mean_square = jnp.mean(head_input * head_input, axis=-1, keepdims=True)
    normed = (
        head_input * lax.rsqrt(mean_square + norm_eps) * final_gain.astype(jnp.float32)
    ).astype(jnp.bfloat16)
    logits = jnp.dot(normed, head_weight, preferred_element_type=jnp.float32)
    local_max = jnp.max(logits, axis=-1)
    local_sum = jnp.sum(jnp.exp(logits - local_max[:, None]), axis=-1)
    stats = lax.all_gather(jnp.stack([local_max, local_sum], -1), ("seq", "tp"), axis=0)
    global_max = jnp.max(stats[..., 0], axis=0)
    global_sum = jnp.sum(stats[..., 1] * jnp.exp(stats[..., 0] - global_max[None]), axis=0)
    log_probs = logits - (global_max + jnp.log(global_sum))[:, None]
    return (prefill_out, decode_out, log_probs)


def solution(mesh):
    return jax.shard_map(
        local,
        mesh=mesh,
        in_specs=(
            P("seq", "tp"),
            P("seq", "tp"),
            P(None, "seq", "tp"),
            P(None, "seq", None, "tp"),
            P(),
            P(None, "tp"),
            P(None, "tp"),
            P(None, None, "tp"),
            P(None, None, "seq", "tp"),
            P(),
            P(),
            P("tp", "seq"),
            P(),
            P(None, ("seq", "tp")),
        ),
        out_specs=(P("seq", "tp"), P(None, "tp"), P(None, ("seq", "tp"))),
        check_vma=False,
    )
```

```python
import math

import jax
import jax.numpy as jnp
from jax import lax
from jax.sharding import PartitionSpec as P

QUERY_HEADS = 40
KEY_HEADS = 8
HEAD_SIZE = 128


neg_large = -1e30
exact = lax.Precision.HIGHEST
norm_eps = 1e-06


def local(
    prefill_hidden,
    prefill_query_rows,
    prefill_key_value,
    request_prefix_cache,
    prefix_lengths,
    decode_hidden,
    decode_query_rows,
    decode_kv,
    decode_slot_cache,
    cache_lengths,
    slot_table,
    out_weight,
    final_gain,
    head_weight,
):
    query_group_width = QUERY_HEADS // KEY_HEADS
    score_scale = 1.0 / math.sqrt(HEAD_SIZE)
    kv_local = prefill_key_value.shape[2] // HEAD_SIZE
    seq_index = lax.axis_index("seq")
    tp_index = lax.axis_index("tp")
    n_seq = lax.axis_size("seq")
    n_tp = lax.axis_size("tp")
    span_len = prefill_query_rows.shape[0]
    prefix_len = request_prefix_cache.shape[2]
    feature_width = prefill_hidden.shape[1]
    model_width = feature_width * n_tp
    column_width = out_weight.shape[1]
    decode_count = decode_query_rows.shape[0]

    ctx_local = decode_slot_cache.shape[2]
    chosen = jnp.take(decode_slot_cache, slot_table, axis=1)
    positions = seq_index * ctx_local + jnp.arange(ctx_local)
    decode_live = (positions[None, :] < cache_lengths[:, None])[:, None, None, :]
    decode_token_rows = decode_query_rows.reshape(
        decode_count, kv_local, query_group_width, HEAD_SIZE
    )
    cache_keys = chosen[0].reshape(decode_count, ctx_local, kv_local, HEAD_SIZE)
    cache_values = chosen[1].reshape(decode_count, ctx_local, kv_local, HEAD_SIZE)
    decode_scores = (
        jnp.einsum(
            "bkgh,bskh->bkgs", decode_token_rows, cache_keys, preferred_element_type=jnp.float32
        )
        * score_scale
    )
    decode_masked = jnp.where(decode_live, decode_scores, neg_large)
    decode_max = jnp.max(decode_masked, axis=-1).astype(jnp.bfloat16).astype(jnp.float32)
    decode_weights = jnp.where(decode_live, jnp.exp(decode_masked - decode_max[..., None]), 0.0)
    decode_sum = jnp.sum(decode_weights, axis=-1)
    decode_mixed = jnp.einsum(
        "bkgs,bskh->bkgh", decode_weights, cache_values.astype(jnp.float32), precision=exact
    )
    prefix_end = lax.dynamic_slice_in_dim(prefix_lengths, seq_index, 1)[0]
    query_matrix = prefill_query_rows.reshape(span_len, kv_local, query_group_width, HEAD_SIZE)
    joined_keys = jnp.concatenate([request_prefix_cache[0, 0], prefill_key_value[0]], 0).reshape(
        prefix_len + span_len, kv_local, HEAD_SIZE
    )
    value_matrix = jnp.concatenate([request_prefix_cache[1, 0], prefill_key_value[1]], 0).reshape(
        prefix_len + span_len, kv_local, HEAD_SIZE
    )
    key_place = jnp.arange(prefix_len + span_len)
    query_place = jnp.arange(span_len)
    live_mask = jnp.where(
        key_place[None, :] < prefix_len,
        key_place[None, :] < prefix_end,
        key_place[None, :] - prefix_len <= query_place[:, None],
    )
    scores = (
        jnp.einsum("rkgh,skh->kgrs", query_matrix, joined_keys, preferred_element_type=jnp.float32)
        * score_scale
    )
    masked = jnp.where(live_mask, scores, neg_large)
    row_max = jnp.max(masked, axis=-1, keepdims=True)
    weights = jnp.where(live_mask, jnp.exp(masked - row_max), 0.0)
    row_sum = jnp.sum(weights, axis=-1)
    weights_low = weights.astype(jnp.bfloat16)
    mixed = jnp.einsum(
        "kgrs,skh->rkgh", weights_low, value_matrix, preferred_element_type=jnp.float32
    )
    prefill_attention = (
        (mixed / jnp.transpose(row_sum, (2, 0, 1))[..., None])
        .astype(jnp.bfloat16)
        .reshape(span_len, -1)
    )
    sum_high = decode_sum.astype(jnp.bfloat16)
    sum_low = (decode_sum - sum_high.astype(jnp.float32)).astype(jnp.bfloat16)
    mixed_high = decode_mixed.astype(jnp.bfloat16)
    mixed_low = (decode_mixed - mixed_high.astype(jnp.float32)).astype(jnp.bfloat16)
    stat_count = decode_sum.size
    decode_flat = jnp.concatenate(
        [
            decode_max.astype(jnp.bfloat16).reshape(-1),
            sum_high.reshape(-1),
            sum_low.reshape(-1),
            mixed_high.reshape(-1),
            mixed_low.reshape(-1),
        ]
    )
    extra_rows = -(-decode_flat.size // feature_width)
    decode_flat = jnp.pad(decode_flat, (0, extra_rows * feature_width - decode_flat.size))
    payload_rows = jnp.concatenate(
        [
            prefill_attention,
            prefill_hidden[span_len - 1 :],
            decode_flat.reshape(extra_rows, feature_width),
        ],
        0,
    )
    gathered = lax.all_gather(payload_rows, "seq", axis=0)
    every_row = gathered[:, :span_len].reshape(n_seq * span_len, feature_width)
    last_hidden = gathered[:, span_len].astype(jnp.float32)
    every_flat = gathered[:, span_len + 1 :].reshape(n_seq, -1).astype(jnp.float32)
    mixed_count = decode_mixed.size
    part_max = every_flat[:, :stat_count].reshape((n_seq,) + decode_sum.shape)
    part_sum = (
        every_flat[:, stat_count : 2 * stat_count] + every_flat[:, 2 * stat_count : 3 * stat_count]
    ).reshape((n_seq,) + decode_sum.shape)
    mixed_at = 3 * stat_count
    part_mixed = (
        every_flat[:, mixed_at : mixed_at + mixed_count]
        + every_flat[:, mixed_at + mixed_count : mixed_at + 2 * mixed_count]
    ).reshape((n_seq,) + decode_mixed.shape)

    best = jnp.max(part_max, axis=0)
    factors = jnp.exp(part_max - best[None])
    totals = jnp.sum(part_sum * factors, axis=0)
    mixtures = jnp.sum(part_mixed * factors[..., None], axis=0)
    own_keys = decode_kv[0].reshape(decode_count, kv_local, HEAD_SIZE)
    own_values = decode_kv[1].reshape(decode_count, kv_local, HEAD_SIZE).astype(jnp.float32)
    own_scores = (
        jnp.einsum("bkgh,bkh->bkg", decode_token_rows, own_keys, preferred_element_type=jnp.float32)
        * score_scale
    )
    final_max = jnp.maximum(best, own_scores)
    factor_one = jnp.exp(best - final_max)
    factor_two = jnp.exp(own_scores - final_max)
    final_sum = totals * factor_one + factor_two
    final_mixed = mixtures * factor_one[..., None] + own_values[:, :, None, :] * factor_two[..., None]
    decode_attention = (
        (final_mixed / final_sum[..., None]).astype(jnp.bfloat16).reshape(decode_count, -1)
    )

    attention_all = jnp.concatenate([every_row, decode_attention], 0)
    column_block = jnp.dot(attention_all, out_weight, preferred_element_type=jnp.float32)
    prefill_block = column_block[: n_seq * span_len].reshape(n_seq, span_len, column_width)

    blocks_per_tp = n_seq // n_tp
    owner_tp = seq_index // blocks_per_tp
    column_start = (seq_index % blocks_per_tp) * column_width
    decode_hidden_cols = lax.dynamic_slice_in_dim(
        decode_hidden, column_start, column_width, axis=1
    ).astype(jnp.float32)
    last_hidden_cols = lax.dynamic_slice_in_dim(last_hidden, column_start, column_width, axis=1)
    head_hidden_cols = jnp.concatenate([decode_hidden_cols, last_hidden_cols], 0)
    head_part = jnp.concatenate(
        [column_block[n_seq * span_len :], prefill_block[:, span_len - 1]], 0
    )
    head_part = jnp.where(owner_tp == tp_index, head_part + head_hidden_cols, head_part)
    head_all = lax.all_gather(head_part, ("seq", "tp"), axis=0)
    head_rows_count = decode_count + n_seq
    head_all = head_all.reshape(n_seq, n_tp, head_rows_count, column_width)
    head_sum = jnp.sum(head_all, axis=1)
    head_sum = jnp.transpose(head_sum, (1, 0, 2)).reshape(head_rows_count, model_width)
    head_updated = head_sum.astype(jnp.bfloat16)
    decode_out = lax.dynamic_slice_in_dim(
        head_updated[:decode_count], tp_index * feature_width, feature_width, axis=1
    )

    rows_part = span_len // n_tp
    summed_rows = lax.psum_scatter(prefill_block, "tp", scatter_dimension=1, tiled=True)
    by_source = lax.all_to_all(summed_rows, "seq", split_axis=0, concat_axis=0, tiled=True)
    own_columns = lax.all_to_all(by_source, "tp", split_axis=0, concat_axis=1, tiled=True)
    projected = jnp.transpose(own_columns, (1, 0, 2)).reshape(span_len, feature_width)
    del rows_part
    prefill_out = (prefill_hidden.astype(jnp.float32) + projected).astype(jnp.bfloat16)

    head_input = head_updated.astype(jnp.float32)
    mean_square = jnp.mean(head_input * head_input, axis=-1, keepdims=True)
    normed = (
        head_input * lax.rsqrt(mean_square + norm_eps) * final_gain.astype(jnp.float32)
    ).astype(jnp.bfloat16)
    logits = jnp.dot(normed, head_weight, preferred_element_type=jnp.float32)
    local_max = jnp.max(logits, axis=-1)
    local_sum = jnp.sum(jnp.exp(logits - local_max[:, None]), axis=-1)
    stats = lax.all_gather(jnp.stack([local_max, local_sum], -1), ("seq", "tp"), axis=0)
    global_max = jnp.max(stats[..., 0], axis=0)
    global_sum = jnp.sum(stats[..., 1] * jnp.exp(stats[..., 0] - global_max[None]), axis=0)
    log_probs = logits - (global_max + jnp.log(global_sum))[:, None]
    return (prefill_out, decode_out, log_probs)


def solution(mesh):
    return jax.shard_map(
        local,
        mesh=mesh,
        in_specs=(
            P("seq", "tp"),
            P("seq", "tp"),
            P(None, "seq", "tp"),
            P(None, "seq", None, "tp"),
            P(),
            P(None, "tp"),
            P(None, "tp"),
            P(None, None, "tp"),
            P(None, None, "seq", "tp"),
            P(),
            P(),
            P("tp", "seq"),
            P(),
            P(None, ("seq", "tp")),
        ),
        out_specs=(P("seq", "tp"), P(None, "tp"), P(None, ("seq", "tp"))),
        check_vma=False,
    )
```

```python
import math

import jax
import jax.numpy as jnp
from jax import lax
from jax.sharding import PartitionSpec as P

QUERY_HEADS = 40
KEY_HEADS = 8
HEAD_SIZE = 128


neg_large = -1e30
exact = lax.Precision.HIGHEST
norm_eps = 1e-06


def local(
    prefill_hidden,
    prefill_query_rows,
    prefill_key_value,
    request_prefix_cache,
    prefix_lengths,
    decode_hidden,
    decode_query_rows,
    decode_kv,
    decode_slot_cache,
    cache_lengths,
    slot_table,
    out_weight,
    final_gain,
    head_weight,
):
    query_group_width = QUERY_HEADS // KEY_HEADS
    score_scale = 1.0 / math.sqrt(HEAD_SIZE)
    kv_local = prefill_key_value.shape[2] // HEAD_SIZE
    seq_index = lax.axis_index("seq")
    tp_index = lax.axis_index("tp")
    n_seq = lax.axis_size("seq")
    n_tp = lax.axis_size("tp")
    span_len = prefill_query_rows.shape[0]
    prefix_len = request_prefix_cache.shape[2]
    feature_width = prefill_hidden.shape[1]
    model_width = feature_width * n_tp
    column_width = out_weight.shape[1]
    decode_count = decode_query_rows.shape[0]

    ctx_local = decode_slot_cache.shape[2]
    chosen = jnp.take(decode_slot_cache, slot_table, axis=1)
    positions = seq_index * ctx_local + jnp.arange(ctx_local)
    decode_live = (positions[None, :] < cache_lengths[:, None])[:, None, None, :]
    decode_token_rows = decode_query_rows.reshape(
        decode_count, kv_local, query_group_width, HEAD_SIZE
    )
    cache_keys = chosen[0].reshape(decode_count, ctx_local, kv_local, HEAD_SIZE)
    cache_values = chosen[1].reshape(decode_count, ctx_local, kv_local, HEAD_SIZE)
    decode_scores = (
        jnp.einsum(
            "bkgh,bskh->bkgs", decode_token_rows, cache_keys, preferred_element_type=jnp.float32
        )
        * score_scale
    )
    decode_masked = jnp.where(decode_live, decode_scores, neg_large)
    decode_max = jnp.max(decode_masked, axis=-1).astype(jnp.bfloat16).astype(jnp.float32)
    decode_weights = jnp.where(decode_live, jnp.exp(decode_masked - decode_max[..., None]), 0.0)
    decode_sum = jnp.sum(decode_weights, axis=-1)
    decode_mixed = jnp.einsum(
        "bkgs,bskh->bkgh", decode_weights, cache_values.astype(jnp.float32), precision=exact
    )
    prefix_end = lax.dynamic_slice_in_dim(prefix_lengths, seq_index, 1)[0]
    query_matrix = prefill_query_rows.reshape(span_len, kv_local, query_group_width, HEAD_SIZE)
    joined_keys = jnp.concatenate([request_prefix_cache[0, 0], prefill_key_value[0]], 0).reshape(
        prefix_len + span_len, kv_local, HEAD_SIZE
    )
    value_matrix = jnp.concatenate([request_prefix_cache[1, 0], prefill_key_value[1]], 0).reshape(
        prefix_len + span_len, kv_local, HEAD_SIZE
    )
    key_place = jnp.arange(prefix_len + span_len)
    query_place = jnp.arange(span_len)
    live_mask = jnp.where(
        key_place[None, :] < prefix_len,
        key_place[None, :] < prefix_end,
        key_place[None, :] - prefix_len <= query_place[:, None],
    )
    scores = (
        jnp.einsum("rkgh,skh->kgrs", query_matrix, joined_keys, preferred_element_type=jnp.float32)
        * score_scale
    )
    masked = jnp.where(live_mask, scores, neg_large)
    row_max = jnp.max(masked, axis=-1, keepdims=True)
    weights = jnp.where(live_mask, jnp.exp(masked - row_max), 0.0)
    row_sum = jnp.sum(weights, axis=-1)
    weights_low = weights.astype(jnp.bfloat16)
    mixed = jnp.einsum(
        "kgrs,skh->rkgh", weights_low, value_matrix, preferred_element_type=jnp.float32
    )
    prefill_attention = (
        (mixed / jnp.transpose(row_sum, (2, 0, 1))[..., None])
        .astype(jnp.bfloat16)
        .reshape(span_len, -1)
    )
    sum_high = decode_sum.astype(jnp.bfloat16)
    sum_low = (decode_sum - sum_high.astype(jnp.float32)).astype(jnp.bfloat16)
    mixed_high = decode_mixed.astype(jnp.bfloat16)
    mixed_low = (decode_mixed - mixed_high.astype(jnp.float32)).astype(jnp.bfloat16)
    stat_count = decode_sum.size
    decode_flat = jnp.concatenate(
        [
            decode_max.astype(jnp.bfloat16).reshape(-1),
            sum_high.reshape(-1),
            sum_low.reshape(-1),
            mixed_high.reshape(-1),
            mixed_low.reshape(-1),
        ]
    )
    extra_rows = -(-decode_flat.size // feature_width)
    decode_flat = jnp.pad(decode_flat, (0, extra_rows * feature_width - decode_flat.size))
    small_rows = jnp.concatenate(
        [
            prefill_attention[span_len - 1 :],
            prefill_hidden[span_len - 1 :],
            decode_flat.reshape(extra_rows, feature_width),
        ],
        0,
    )
    small_gathered = lax.all_gather(small_rows, "seq", axis=0)
    every_row = lax.all_gather(prefill_attention, "seq", axis=0).reshape(n_seq * span_len, feature_width)
    last_attention = small_gathered[:, 0]
    last_hidden = small_gathered[:, 1].astype(jnp.float32)
    every_flat = small_gathered[:, 2:].reshape(n_seq, -1).astype(jnp.float32)
    mixed_count = decode_mixed.size
    part_max = every_flat[:, :stat_count].reshape((n_seq,) + decode_sum.shape)
    part_sum = (
        every_flat[:, stat_count : 2 * stat_count] + every_flat[:, 2 * stat_count : 3 * stat_count]
    ).reshape((n_seq,) + decode_sum.shape)
    mixed_at = 3 * stat_count
    part_mixed = (
        every_flat[:, mixed_at : mixed_at + mixed_count]
        + every_flat[:, mixed_at + mixed_count : mixed_at + 2 * mixed_count]
    ).reshape((n_seq,) + decode_mixed.shape)

    best = jnp.max(part_max, axis=0)
    factors = jnp.exp(part_max - best[None])
    totals = jnp.sum(part_sum * factors, axis=0)
    mixtures = jnp.sum(part_mixed * factors[..., None], axis=0)
    own_keys = decode_kv[0].reshape(decode_count, kv_local, HEAD_SIZE)
    own_values = decode_kv[1].reshape(decode_count, kv_local, HEAD_SIZE).astype(jnp.float32)
    own_scores = (
        jnp.einsum("bkgh,bkh->bkg", decode_token_rows, own_keys, preferred_element_type=jnp.float32)
        * score_scale
    )
    final_max = jnp.maximum(best, own_scores)
    factor_one = jnp.exp(best - final_max)
    factor_two = jnp.exp(own_scores - final_max)
    final_sum = totals * factor_one + factor_two
    final_mixed = mixtures * factor_one[..., None] + own_values[:, :, None, :] * factor_two[..., None]
    decode_attention = (
        (final_mixed / final_sum[..., None]).astype(jnp.bfloat16).reshape(decode_count, -1)
    )

    blocks_per_tp = n_seq // n_tp
    owner_tp = seq_index // blocks_per_tp
    column_start = (seq_index % blocks_per_tp) * column_width
    decode_hidden_cols = lax.dynamic_slice_in_dim(
        decode_hidden, column_start, column_width, axis=1
    ).astype(jnp.float32)
    last_hidden_cols = lax.dynamic_slice_in_dim(last_hidden, column_start, column_width, axis=1)
    head_hidden_cols = jnp.concatenate([decode_hidden_cols, last_hidden_cols], 0)
    head_attention = jnp.concatenate([decode_attention, last_attention], 0)
    head_part = jnp.dot(head_attention, out_weight, preferred_element_type=jnp.float32)
    head_part = jnp.where(owner_tp == tp_index, head_part + head_hidden_cols, head_part)
    head_all = lax.all_gather(head_part, ("seq", "tp"), axis=0)
    head_rows_count = decode_count + n_seq
    head_all = head_all.reshape(n_seq, n_tp, head_rows_count, column_width)
    head_sum = jnp.sum(head_all, axis=1)
    head_sum = jnp.transpose(head_sum, (1, 0, 2)).reshape(head_rows_count, model_width)
    head_updated = head_sum.astype(jnp.bfloat16)
    decode_out = lax.dynamic_slice_in_dim(
        head_updated[:decode_count], tp_index * feature_width, feature_width, axis=1
    )

    head_input = head_updated.astype(jnp.float32)
    mean_square = jnp.mean(head_input * head_input, axis=-1, keepdims=True)
    normed = (
        head_input * lax.rsqrt(mean_square + norm_eps) * final_gain.astype(jnp.float32)
    ).astype(jnp.bfloat16)
    logits = jnp.dot(normed, head_weight, preferred_element_type=jnp.float32)
    local_max = jnp.max(logits, axis=-1)
    local_sum = jnp.sum(jnp.exp(logits - local_max[:, None]), axis=-1)
    stats = lax.all_gather(jnp.stack([local_max, local_sum], -1), ("seq", "tp"), axis=0)
    global_max = jnp.max(stats[..., 0], axis=0)
    global_sum = jnp.sum(stats[..., 1] * jnp.exp(stats[..., 0] - global_max[None]), axis=0)
    log_probs = logits - (global_max + jnp.log(global_sum))[:, None]
    every_row, decode_out, log_probs = lax.optimization_barrier((every_row, decode_out, log_probs))

    column_block = jnp.dot(every_row, out_weight, preferred_element_type=jnp.float32)
    prefill_block = column_block.reshape(n_seq, span_len, column_width)

    summed_rows = lax.psum_scatter(prefill_block, "tp", scatter_dimension=1, tiled=True)
    by_source = lax.all_to_all(summed_rows, "seq", split_axis=0, concat_axis=0, tiled=True)
    own_columns = lax.all_to_all(by_source, "tp", split_axis=0, concat_axis=1, tiled=True)
    projected = jnp.transpose(own_columns, (1, 0, 2)).reshape(span_len, feature_width)
    prefill_out = (prefill_hidden.astype(jnp.float32) + projected).astype(jnp.bfloat16)

    return (prefill_out, decode_out, log_probs)


def solution(mesh):
    return jax.shard_map(
        local,
        mesh=mesh,
        in_specs=(
            P("seq", "tp"),
            P("seq", "tp"),
            P(None, "seq", "tp"),
            P(None, "seq", None, "tp"),
            P(),
            P(None, "tp"),
            P(None, "tp"),
            P(None, None, "tp"),
            P(None, None, "seq", "tp"),
            P(),
            P(),
            P("tp", "seq"),
            P(),
            P(None, ("seq", "tp")),
        ),
        out_specs=(P("seq", "tp"), P(None, "tp"), P(None, ("seq", "tp"))),
        check_vma=False,
    )
```

```python
import math

import jax
import jax.numpy as jnp
from jax import lax
from jax.sharding import PartitionSpec as P

QUERY_HEADS = 40
KEY_HEADS = 8
HEAD_SIZE = 128


neg_large = -1e30
exact = lax.Precision.HIGHEST
norm_eps = 1e-06


def local(
    prefill_hidden,
    prefill_query_rows,
    prefill_key_value,
    request_prefix_cache,
    prefix_lengths,
    decode_hidden,
    decode_query_rows,
    decode_kv,
    decode_slot_cache,
    cache_lengths,
    slot_table,
    out_weight,
    final_gain,
    head_weight,
):
    query_group_width = QUERY_HEADS // KEY_HEADS
    score_scale = 1.0 / math.sqrt(HEAD_SIZE)
    kv_local = prefill_key_value.shape[2] // HEAD_SIZE
    seq_index = lax.axis_index("seq")
    tp_index = lax.axis_index("tp")
    n_seq = lax.axis_size("seq")
    n_tp = lax.axis_size("tp")
    span_len = prefill_query_rows.shape[0]
    prefix_len = request_prefix_cache.shape[2]
    feature_width = prefill_hidden.shape[1]
    model_width = feature_width * n_tp
    column_width = out_weight.shape[1]
    decode_count = decode_query_rows.shape[0]

    ctx_local = decode_slot_cache.shape[2]
    chosen = jnp.take(decode_slot_cache, slot_table, axis=1)
    positions = seq_index * ctx_local + jnp.arange(ctx_local)
    decode_live = (positions[None, :] < cache_lengths[:, None])[:, None, None, :]
    decode_token_rows = decode_query_rows.reshape(
        decode_count, kv_local, query_group_width, HEAD_SIZE
    )
    cache_keys = chosen[0].reshape(decode_count, ctx_local, kv_local, HEAD_SIZE)
    cache_values = chosen[1].reshape(decode_count, ctx_local, kv_local, HEAD_SIZE)
    decode_scores = (
        jnp.einsum(
            "bkgh,bskh->bkgs", decode_token_rows, cache_keys, preferred_element_type=jnp.float32
        )
        * score_scale
    )
    decode_masked = jnp.where(decode_live, decode_scores, neg_large)
    decode_max = jnp.max(decode_masked, axis=-1).astype(jnp.bfloat16).astype(jnp.float32)
    decode_weights = jnp.where(decode_live, jnp.exp(decode_masked - decode_max[..., None]), 0.0)
    decode_sum = jnp.sum(decode_weights, axis=-1)
    decode_mixed = jnp.einsum(
        "bkgs,bskh->bkgh", decode_weights, cache_values.astype(jnp.float32), precision=exact
    )
    prefix_end = lax.dynamic_slice_in_dim(prefix_lengths, seq_index, 1)[0]
    query_matrix = prefill_query_rows.reshape(span_len, kv_local, query_group_width, HEAD_SIZE)
    joined_keys = jnp.concatenate([request_prefix_cache[0, 0], prefill_key_value[0]], 0).reshape(
        prefix_len + span_len, kv_local, HEAD_SIZE
    )
    value_matrix = jnp.concatenate([request_prefix_cache[1, 0], prefill_key_value[1]], 0).reshape(
        prefix_len + span_len, kv_local, HEAD_SIZE
    )
    key_place = jnp.arange(prefix_len + span_len)
    query_place = jnp.arange(span_len)
    live_mask = jnp.where(
        key_place[None, :] < prefix_len,
        key_place[None, :] < prefix_end,
        key_place[None, :] - prefix_len <= query_place[:, None],
    )
    scores = (
        jnp.einsum("rkgh,skh->kgrs", query_matrix, joined_keys, preferred_element_type=jnp.float32)
        * score_scale
    )
    masked = jnp.where(live_mask, scores, neg_large)
    row_max = jnp.max(masked, axis=-1, keepdims=True)
    weights = jnp.where(live_mask, jnp.exp(masked - row_max), 0.0)
    row_sum = jnp.sum(weights, axis=-1)
    weights_low = weights.astype(jnp.bfloat16)
    mixed = jnp.einsum(
        "kgrs,skh->rkgh", weights_low, value_matrix, preferred_element_type=jnp.float32
    )
    prefill_attention = (
        (mixed / jnp.transpose(row_sum, (2, 0, 1))[..., None])
        .astype(jnp.bfloat16)
        .reshape(span_len, -1)
    )
    sum_high = decode_sum.astype(jnp.bfloat16)
    sum_low = (decode_sum - sum_high.astype(jnp.float32)).astype(jnp.bfloat16)
    mixed_high = decode_mixed.astype(jnp.bfloat16)
    mixed_low = (decode_mixed - mixed_high.astype(jnp.float32)).astype(jnp.bfloat16)
    stat_count = decode_sum.size
    decode_flat = jnp.concatenate(
        [
            decode_max.astype(jnp.bfloat16).reshape(-1),
            sum_high.reshape(-1),
            sum_low.reshape(-1),
            mixed_high.reshape(-1),
            mixed_low.reshape(-1),
        ]
    )
    extra_rows = -(-decode_flat.size // feature_width)
    decode_flat = jnp.pad(decode_flat, (0, extra_rows * feature_width - decode_flat.size))
    small_rows = jnp.concatenate(
        [
            prefill_attention[span_len - 1 :],
            prefill_hidden[span_len - 1 :],
            decode_flat.reshape(extra_rows, feature_width),
        ],
        0,
    )
    small_gathered = lax.all_gather(small_rows, "seq", axis=0)
    every_row = lax.all_gather(prefill_attention, "seq", axis=0).reshape(n_seq * span_len, feature_width)
    last_attention = small_gathered[:, 0]
    last_hidden = small_gathered[:, 1].astype(jnp.float32)
    every_flat = small_gathered[:, 2:].reshape(n_seq, -1).astype(jnp.float32)
    mixed_count = decode_mixed.size
    part_max = every_flat[:, :stat_count].reshape((n_seq,) + decode_sum.shape)
    part_sum = (
        every_flat[:, stat_count : 2 * stat_count] + every_flat[:, 2 * stat_count : 3 * stat_count]
    ).reshape((n_seq,) + decode_sum.shape)
    mixed_at = 3 * stat_count
    part_mixed = (
        every_flat[:, mixed_at : mixed_at + mixed_count]
        + every_flat[:, mixed_at + mixed_count : mixed_at + 2 * mixed_count]
    ).reshape((n_seq,) + decode_mixed.shape)

    best = jnp.max(part_max, axis=0)
    factors = jnp.exp(part_max - best[None])
    totals = jnp.sum(part_sum * factors, axis=0)
    mixtures = jnp.sum(part_mixed * factors[..., None], axis=0)
    own_keys = decode_kv[0].reshape(decode_count, kv_local, HEAD_SIZE)
    own_values = decode_kv[1].reshape(decode_count, kv_local, HEAD_SIZE).astype(jnp.float32)
    own_scores = (
        jnp.einsum("bkgh,bkh->bkg", decode_token_rows, own_keys, preferred_element_type=jnp.float32)
        * score_scale
    )
    final_max = jnp.maximum(best, own_scores)
    factor_one = jnp.exp(best - final_max)
    factor_two = jnp.exp(own_scores - final_max)
    final_sum = totals * factor_one + factor_two
    final_mixed = mixtures * factor_one[..., None] + own_values[:, :, None, :] * factor_two[..., None]
    decode_attention = (
        (final_mixed / final_sum[..., None]).astype(jnp.bfloat16).reshape(decode_count, -1)
    )

    blocks_per_tp = n_seq // n_tp
    owner_tp = seq_index // blocks_per_tp
    column_start = (seq_index % blocks_per_tp) * column_width
    decode_hidden_cols = lax.dynamic_slice_in_dim(
        decode_hidden, column_start, column_width, axis=1
    ).astype(jnp.float32)
    last_hidden_cols = lax.dynamic_slice_in_dim(last_hidden, column_start, column_width, axis=1)
    head_hidden_cols = jnp.concatenate([decode_hidden_cols, last_hidden_cols], 0)
    head_attention = jnp.concatenate([decode_attention, last_attention], 0)
    head_part = jnp.dot(head_attention, out_weight, preferred_element_type=jnp.float32)
    head_part = jnp.where(owner_tp == tp_index, head_part + head_hidden_cols, head_part)
    head_all = lax.all_gather(head_part, ("seq", "tp"), axis=0)
    head_rows_count = decode_count + n_seq
    head_all = head_all.reshape(n_seq, n_tp, head_rows_count, column_width)
    head_sum = jnp.sum(head_all, axis=1)
    head_sum = jnp.transpose(head_sum, (1, 0, 2)).reshape(head_rows_count, model_width)
    head_updated = head_sum.astype(jnp.bfloat16)
    decode_out = lax.dynamic_slice_in_dim(
        head_updated[:decode_count], tp_index * feature_width, feature_width, axis=1
    )

    head_input = head_updated.astype(jnp.float32)
    mean_square = jnp.mean(head_input * head_input, axis=-1, keepdims=True)
    normed = (
        head_input * lax.rsqrt(mean_square + norm_eps) * final_gain.astype(jnp.float32)
    ).astype(jnp.bfloat16)
    logits = jnp.dot(normed, head_weight, preferred_element_type=jnp.float32)
    local_max = jnp.max(logits, axis=-1)
    local_sum = jnp.sum(jnp.exp(logits - local_max[:, None]), axis=-1)
    local_stats = jnp.stack([local_max, local_sum], -1)
    every_row, local_stats = lax.optimization_barrier((every_row, local_stats))
    column_block = jnp.dot(every_row, out_weight, preferred_element_type=jnp.float32)
    prefill_block = column_block.reshape(n_seq, span_len, column_width)

    summed_rows = lax.psum_scatter(prefill_block, "tp", scatter_dimension=1, tiled=True)
    summed_rows, local_stats = lax.optimization_barrier((summed_rows, local_stats))
    by_source = lax.all_to_all(summed_rows, "seq", split_axis=0, concat_axis=0, tiled=True)
    own_columns = lax.all_to_all(by_source, "tp", split_axis=0, concat_axis=1, tiled=True)
    projected = jnp.transpose(own_columns, (1, 0, 2)).reshape(span_len, feature_width)
    prefill_out = (prefill_hidden.astype(jnp.float32) + projected).astype(jnp.bfloat16)

    stats = lax.all_gather(local_stats, ("seq", "tp"), axis=0)
    global_max = jnp.max(stats[..., 0], axis=0)
    global_sum = jnp.sum(stats[..., 1] * jnp.exp(stats[..., 0] - global_max[None]), axis=0)
    log_probs = logits - (global_max + jnp.log(global_sum))[:, None]

    return (prefill_out, decode_out, log_probs)


def solution(mesh):
    return jax.shard_map(
        local,
        mesh=mesh,
        in_specs=(
            P("seq", "tp"),
            P("seq", "tp"),
            P(None, "seq", "tp"),
            P(None, "seq", None, "tp"),
            P(),
            P(None, "tp"),
            P(None, "tp"),
            P(None, None, "tp"),
            P(None, None, "seq", "tp"),
            P(),
            P(),
            P("tp", "seq"),
            P(),
            P(None, ("seq", "tp")),
        ),
        out_specs=(P("seq", "tp"), P(None, "tp"), P(None, ("seq", "tp"))),
        check_vma=False,
    )
```

```python
import math

import jax
import jax.numpy as jnp
from jax import lax
from jax.sharding import PartitionSpec as P

QUERY_HEADS = 40
KEY_HEADS = 8
HEAD_SIZE = 128


neg_large = -1e30
exact = lax.Precision.HIGHEST
norm_eps = 1e-06


def doubling_gather(value, axis):
    count = lax.axis_size(axis)
    if count & (count - 1):
        return lax.all_gather(value, axis, axis=0)
    index = lax.axis_index(axis)
    block = value[None]
    distance = 1
    while distance < count:
        pairs = [(i, i ^ distance) for i in range(count)]
        other = lax.ppermute(block, axis, pairs)
        low = (index & distance) == 0
        block = jnp.where(
            low, jnp.concatenate([block, other], 0), jnp.concatenate([other, block], 0)
        )
        distance *= 2
    return block


def local(
    prefill_hidden,
    prefill_query_rows,
    prefill_key_value,
    request_prefix_cache,
    prefix_lengths,
    decode_hidden,
    decode_query_rows,
    decode_kv,
    decode_slot_cache,
    cache_lengths,
    slot_table,
    out_weight,
    final_gain,
    head_weight,
):
    query_group_width = QUERY_HEADS // KEY_HEADS
    score_scale = 1.0 / math.sqrt(HEAD_SIZE)
    kv_local = prefill_key_value.shape[2] // HEAD_SIZE
    seq_index = lax.axis_index("seq")
    tp_index = lax.axis_index("tp")
    n_seq = lax.axis_size("seq")
    n_tp = lax.axis_size("tp")
    span_len = prefill_query_rows.shape[0]
    prefix_len = request_prefix_cache.shape[2]
    feature_width = prefill_hidden.shape[1]
    model_width = feature_width * n_tp
    column_width = out_weight.shape[1]
    decode_count = decode_query_rows.shape[0]

    ctx_local = decode_slot_cache.shape[2]
    chosen = jnp.take(decode_slot_cache, slot_table, axis=1)
    positions = seq_index * ctx_local + jnp.arange(ctx_local)
    decode_live = (positions[None, :] < cache_lengths[:, None])[:, None, None, :]
    decode_token_rows = decode_query_rows.reshape(
        decode_count, kv_local, query_group_width, HEAD_SIZE
    )
    cache_keys = chosen[0].reshape(decode_count, ctx_local, kv_local, HEAD_SIZE)
    cache_values = chosen[1].reshape(decode_count, ctx_local, kv_local, HEAD_SIZE)
    decode_scores = (
        jnp.einsum(
            "bkgh,bskh->bkgs", decode_token_rows, cache_keys, preferred_element_type=jnp.float32
        )
        * score_scale
    )
    decode_masked = jnp.where(decode_live, decode_scores, neg_large)
    decode_max = jnp.max(decode_masked, axis=-1).astype(jnp.bfloat16).astype(jnp.float32)
    decode_weights = jnp.where(decode_live, jnp.exp(decode_masked - decode_max[..., None]), 0.0)
    decode_sum = jnp.sum(decode_weights, axis=-1)
    decode_mixed = jnp.einsum(
        "bkgs,bskh->bkgh", decode_weights, cache_values.astype(jnp.float32), precision=exact
    )
    prefix_end = lax.dynamic_slice_in_dim(prefix_lengths, seq_index, 1)[0]
    query_matrix = prefill_query_rows.reshape(span_len, kv_local, query_group_width, HEAD_SIZE)
    joined_keys = jnp.concatenate([request_prefix_cache[0, 0], prefill_key_value[0]], 0).reshape(
        prefix_len + span_len, kv_local, HEAD_SIZE
    )
    value_matrix = jnp.concatenate([request_prefix_cache[1, 0], prefill_key_value[1]], 0).reshape(
        prefix_len + span_len, kv_local, HEAD_SIZE
    )
    key_place = jnp.arange(prefix_len + span_len)
    query_place = jnp.arange(span_len)
    live_mask = jnp.where(
        key_place[None, :] < prefix_len,
        key_place[None, :] < prefix_end,
        key_place[None, :] - prefix_len <= query_place[:, None],
    )
    scores = (
        jnp.einsum("rkgh,skh->kgrs", query_matrix, joined_keys, preferred_element_type=jnp.float32)
        * score_scale
    )
    masked = jnp.where(live_mask, scores, neg_large)
    row_max = jnp.max(masked, axis=-1, keepdims=True)
    weights = jnp.where(live_mask, jnp.exp(masked - row_max), 0.0)
    row_sum = jnp.sum(weights, axis=-1)
    weights_low = weights.astype(jnp.bfloat16)
    mixed = jnp.einsum(
        "kgrs,skh->rkgh", weights_low, value_matrix, preferred_element_type=jnp.float32
    )
    prefill_attention = (
        (mixed / jnp.transpose(row_sum, (2, 0, 1))[..., None])
        .astype(jnp.bfloat16)
        .reshape(span_len, -1)
    )
    sum_high = decode_sum.astype(jnp.bfloat16)
    sum_low = (decode_sum - sum_high.astype(jnp.float32)).astype(jnp.bfloat16)
    mixed_high = decode_mixed.astype(jnp.bfloat16)
    mixed_low = (decode_mixed - mixed_high.astype(jnp.float32)).astype(jnp.bfloat16)
    stat_count = decode_sum.size
    decode_flat = jnp.concatenate(
        [
            decode_max.astype(jnp.bfloat16).reshape(-1),
            sum_high.reshape(-1),
            sum_low.reshape(-1),
            mixed_high.reshape(-1),
            mixed_low.reshape(-1),
        ]
    )
    extra_rows = -(-decode_flat.size // feature_width)
    decode_flat = jnp.pad(decode_flat, (0, extra_rows * feature_width - decode_flat.size))
    small_rows = jnp.concatenate(
        [
            prefill_attention[span_len - 1 :],
            prefill_hidden[span_len - 1 :],
            decode_flat.reshape(extra_rows, feature_width),
        ],
        0,
    )
    small_gathered = doubling_gather(small_rows, "seq")
    every_row = lax.all_gather(prefill_attention, "seq", axis=0).reshape(n_seq * span_len, feature_width)
    last_attention = small_gathered[:, 0]
    last_hidden = small_gathered[:, 1].astype(jnp.float32)
    every_flat = small_gathered[:, 2:].reshape(n_seq, -1).astype(jnp.float32)
    mixed_count = decode_mixed.size
    part_max = every_flat[:, :stat_count].reshape((n_seq,) + decode_sum.shape)
    part_sum = (
        every_flat[:, stat_count : 2 * stat_count] + every_flat[:, 2 * stat_count : 3 * stat_count]
    ).reshape((n_seq,) + decode_sum.shape)
    mixed_at = 3 * stat_count
    part_mixed = (
        every_flat[:, mixed_at : mixed_at + mixed_count]
        + every_flat[:, mixed_at + mixed_count : mixed_at + 2 * mixed_count]
    ).reshape((n_seq,) + decode_mixed.shape)

    best = jnp.max(part_max, axis=0)
    factors = jnp.exp(part_max - best[None])
    totals = jnp.sum(part_sum * factors, axis=0)
    mixtures = jnp.sum(part_mixed * factors[..., None], axis=0)
    own_keys = decode_kv[0].reshape(decode_count, kv_local, HEAD_SIZE)
    own_values = decode_kv[1].reshape(decode_count, kv_local, HEAD_SIZE).astype(jnp.float32)
    own_scores = (
        jnp.einsum("bkgh,bkh->bkg", decode_token_rows, own_keys, preferred_element_type=jnp.float32)
        * score_scale
    )
    final_max = jnp.maximum(best, own_scores)
    factor_one = jnp.exp(best - final_max)
    factor_two = jnp.exp(own_scores - final_max)
    final_sum = totals * factor_one + factor_two
    final_mixed = mixtures * factor_one[..., None] + own_values[:, :, None, :] * factor_two[..., None]
    decode_attention = (
        (final_mixed / final_sum[..., None]).astype(jnp.bfloat16).reshape(decode_count, -1)
    )

    blocks_per_tp = n_seq // n_tp
    owner_tp = seq_index // blocks_per_tp
    column_start = (seq_index % blocks_per_tp) * column_width
    decode_hidden_cols = lax.dynamic_slice_in_dim(
        decode_hidden, column_start, column_width, axis=1
    ).astype(jnp.float32)
    last_hidden_cols = lax.dynamic_slice_in_dim(last_hidden, column_start, column_width, axis=1)
    head_hidden_cols = jnp.concatenate([decode_hidden_cols, last_hidden_cols], 0)
    head_attention = jnp.concatenate([decode_attention, last_attention], 0)
    head_part = jnp.dot(head_attention, out_weight, preferred_element_type=jnp.float32)
    head_part = jnp.where(owner_tp == tp_index, head_part + head_hidden_cols, head_part)
    head_all = doubling_gather(doubling_gather(head_part, "tp"), "seq")
    head_rows_count = decode_count + n_seq
    head_all = head_all.reshape(n_seq, n_tp, head_rows_count, column_width)
    head_sum = jnp.sum(head_all, axis=1)
    head_sum = jnp.transpose(head_sum, (1, 0, 2)).reshape(head_rows_count, model_width)
    head_updated = head_sum.astype(jnp.bfloat16)
    decode_out = lax.dynamic_slice_in_dim(
        head_updated[:decode_count], tp_index * feature_width, feature_width, axis=1
    )

    head_input = head_updated.astype(jnp.float32)
    mean_square = jnp.mean(head_input * head_input, axis=-1, keepdims=True)
    normed = (
        head_input * lax.rsqrt(mean_square + norm_eps) * final_gain.astype(jnp.float32)
    ).astype(jnp.bfloat16)
    logits = jnp.dot(normed, head_weight, preferred_element_type=jnp.float32)
    local_max = jnp.max(logits, axis=-1)
    local_sum = jnp.sum(jnp.exp(logits - local_max[:, None]), axis=-1)
    local_stats = jnp.stack([local_max, local_sum], -1)
    stats = doubling_gather(doubling_gather(local_stats, "tp"), "seq").reshape(
        (n_seq * n_tp,) + local_stats.shape
    )
    global_max = jnp.max(stats[..., 0], axis=0)
    global_sum = jnp.sum(stats[..., 1] * jnp.exp(stats[..., 0] - global_max[None]), axis=0)
    log_probs = logits - (global_max + jnp.log(global_sum))[:, None]
    every_row, decode_out, log_probs = lax.optimization_barrier((every_row, decode_out, log_probs))

    column_block = jnp.dot(every_row, out_weight, preferred_element_type=jnp.float32)
    prefill_block = column_block.reshape(n_seq, span_len, column_width)

    summed_rows = lax.psum_scatter(prefill_block, "tp", scatter_dimension=1, tiled=True)
    by_source = lax.all_to_all(summed_rows, "seq", split_axis=0, concat_axis=0, tiled=True)
    own_columns = lax.all_to_all(by_source, "tp", split_axis=0, concat_axis=1, tiled=True)
    projected = jnp.transpose(own_columns, (1, 0, 2)).reshape(span_len, feature_width)
    prefill_out = (prefill_hidden.astype(jnp.float32) + projected).astype(jnp.bfloat16)


    return (prefill_out, decode_out, log_probs)


def solution(mesh):
    return jax.shard_map(
        local,
        mesh=mesh,
        in_specs=(
            P("seq", "tp"),
            P("seq", "tp"),
            P(None, "seq", "tp"),
            P(None, "seq", None, "tp"),
            P(),
            P(None, "tp"),
            P(None, "tp"),
            P(None, None, "tp"),
            P(None, None, "seq", "tp"),
            P(),
            P(),
            P("tp", "seq"),
            P(),
            P(None, ("seq", "tp")),
        ),
        out_specs=(P("seq", "tp"), P(None, "tp"), P(None, ("seq", "tp"))),
        check_vma=False,
    )
```

```python
import math

import jax
import jax.numpy as jnp
from jax import lax
from jax.sharding import PartitionSpec as P

QUERY_HEADS = 40
KEY_HEADS = 8
HEAD_SIZE = 128


neg_large = -1e30
exact = lax.Precision.HIGHEST
norm_eps = 1e-06


def doubling_gather(value, axis):
    count = lax.axis_size(axis)
    if count & (count - 1):
        return lax.all_gather(value, axis, axis=0)
    index = lax.axis_index(axis)
    block = value[None]
    distance = 1
    while distance < count:
        pairs = [(i, i ^ distance) for i in range(count)]
        other = lax.ppermute(block, axis, pairs)
        low = (index & distance) == 0
        block = jnp.where(
            low, jnp.concatenate([block, other], 0), jnp.concatenate([other, block], 0)
        )
        distance *= 2
    return block


def local(
    prefill_hidden,
    prefill_query_rows,
    prefill_key_value,
    request_prefix_cache,
    prefix_lengths,
    decode_hidden,
    decode_query_rows,
    decode_kv,
    decode_slot_cache,
    cache_lengths,
    slot_table,
    out_weight,
    final_gain,
    head_weight,
):
    query_group_width = QUERY_HEADS // KEY_HEADS
    score_scale = 1.0 / math.sqrt(HEAD_SIZE)
    kv_local = prefill_key_value.shape[2] // HEAD_SIZE
    seq_index = lax.axis_index("seq")
    tp_index = lax.axis_index("tp")
    n_seq = lax.axis_size("seq")
    n_tp = lax.axis_size("tp")
    span_len = prefill_query_rows.shape[0]
    prefix_len = request_prefix_cache.shape[2]
    feature_width = prefill_hidden.shape[1]
    model_width = feature_width * n_tp
    column_width = out_weight.shape[1]
    decode_count = decode_query_rows.shape[0]

    ctx_local = decode_slot_cache.shape[2]
    chosen = jnp.take(decode_slot_cache, slot_table, axis=1)
    positions = seq_index * ctx_local + jnp.arange(ctx_local)
    decode_live = (positions[None, :] < cache_lengths[:, None])[:, None, None, :]
    decode_token_rows = decode_query_rows.reshape(
        decode_count, kv_local, query_group_width, HEAD_SIZE
    )
    cache_keys = chosen[0].reshape(decode_count, ctx_local, kv_local, HEAD_SIZE)
    cache_values = chosen[1].reshape(decode_count, ctx_local, kv_local, HEAD_SIZE)
    decode_scores = (
        jnp.einsum(
            "bkgh,bskh->bkgs", decode_token_rows, cache_keys, preferred_element_type=jnp.float32
        )
        * score_scale
    )
    decode_masked = jnp.where(decode_live, decode_scores, neg_large)
    decode_max = jnp.max(decode_masked, axis=-1).astype(jnp.bfloat16).astype(jnp.float32)
    decode_weights = jnp.where(decode_live, jnp.exp(decode_masked - decode_max[..., None]), 0.0)
    decode_sum = jnp.sum(decode_weights, axis=-1)
    decode_mixed = jnp.einsum(
        "bkgs,bskh->bkgh", decode_weights, cache_values.astype(jnp.float32), precision=exact
    )
    prefix_end = lax.dynamic_slice_in_dim(prefix_lengths, seq_index, 1)[0]
    query_matrix = prefill_query_rows.reshape(span_len, kv_local, query_group_width, HEAD_SIZE)
    joined_keys = jnp.concatenate([request_prefix_cache[0, 0], prefill_key_value[0]], 0).reshape(
        prefix_len + span_len, kv_local, HEAD_SIZE
    )
    value_matrix = jnp.concatenate([request_prefix_cache[1, 0], prefill_key_value[1]], 0).reshape(
        prefix_len + span_len, kv_local, HEAD_SIZE
    )
    key_place = jnp.arange(prefix_len + span_len)
    query_place = jnp.arange(span_len)
    live_mask = jnp.where(
        key_place[None, :] < prefix_len,
        key_place[None, :] < prefix_end,
        key_place[None, :] - prefix_len <= query_place[:, None],
    )
    scores = (
        jnp.einsum("rkgh,skh->kgrs", query_matrix, joined_keys, preferred_element_type=jnp.float32)
        * score_scale
    )
    masked = jnp.where(live_mask, scores, neg_large)
    row_max = jnp.max(masked, axis=-1, keepdims=True)
    weights = jnp.where(live_mask, jnp.exp(masked - row_max), 0.0)
    row_sum = jnp.sum(weights, axis=-1)
    weights_low = weights.astype(jnp.bfloat16)
    mixed = jnp.einsum(
        "kgrs,skh->rkgh", weights_low, value_matrix, preferred_element_type=jnp.float32
    )
    prefill_attention = (
        (mixed / jnp.transpose(row_sum, (2, 0, 1))[..., None])
        .astype(jnp.bfloat16)
        .reshape(span_len, -1)
    )
    sum_high = decode_sum.astype(jnp.bfloat16)
    sum_low = (decode_sum - sum_high.astype(jnp.float32)).astype(jnp.bfloat16)
    mixed_high = decode_mixed.astype(jnp.bfloat16)
    mixed_low = (decode_mixed - mixed_high.astype(jnp.float32)).astype(jnp.bfloat16)
    stat_count = decode_sum.size
    decode_flat = jnp.concatenate(
        [
            decode_max.astype(jnp.bfloat16).reshape(-1),
            sum_high.reshape(-1),
            sum_low.reshape(-1),
            mixed_high.reshape(-1),
            mixed_low.reshape(-1),
        ]
    )
    extra_rows = -(-decode_flat.size // feature_width)
    decode_flat = jnp.pad(decode_flat, (0, extra_rows * feature_width - decode_flat.size))
    small_rows = jnp.concatenate(
        [
            prefill_attention[span_len - 1 :],
            prefill_hidden[span_len - 1 :],
            decode_flat.reshape(extra_rows, feature_width),
        ],
        0,
    )
    small_gathered = lax.all_gather(small_rows, "seq", axis=0)
    every_row = lax.all_gather(prefill_attention, "seq", axis=0).reshape(n_seq * span_len, feature_width)
    last_attention = small_gathered[:, 0]
    last_hidden = small_gathered[:, 1].astype(jnp.float32)
    every_flat = small_gathered[:, 2:].reshape(n_seq, -1).astype(jnp.float32)
    mixed_count = decode_mixed.size
    part_max = every_flat[:, :stat_count].reshape((n_seq,) + decode_sum.shape)
    part_sum = (
        every_flat[:, stat_count : 2 * stat_count] + every_flat[:, 2 * stat_count : 3 * stat_count]
    ).reshape((n_seq,) + decode_sum.shape)
    mixed_at = 3 * stat_count
    part_mixed = (
        every_flat[:, mixed_at : mixed_at + mixed_count]
        + every_flat[:, mixed_at + mixed_count : mixed_at + 2 * mixed_count]
    ).reshape((n_seq,) + decode_mixed.shape)

    best = jnp.max(part_max, axis=0)
    factors = jnp.exp(part_max - best[None])
    totals = jnp.sum(part_sum * factors, axis=0)
    mixtures = jnp.sum(part_mixed * factors[..., None], axis=0)
    own_keys = decode_kv[0].reshape(decode_count, kv_local, HEAD_SIZE)
    own_values = decode_kv[1].reshape(decode_count, kv_local, HEAD_SIZE).astype(jnp.float32)
    own_scores = (
        jnp.einsum("bkgh,bkh->bkg", decode_token_rows, own_keys, preferred_element_type=jnp.float32)
        * score_scale
    )
    final_max = jnp.maximum(best, own_scores)
    factor_one = jnp.exp(best - final_max)
    factor_two = jnp.exp(own_scores - final_max)
    final_sum = totals * factor_one + factor_two
    final_mixed = mixtures * factor_one[..., None] + own_values[:, :, None, :] * factor_two[..., None]
    decode_attention = (
        (final_mixed / final_sum[..., None]).astype(jnp.bfloat16).reshape(decode_count, -1)
    )

    blocks_per_tp = n_seq // n_tp
    owner_tp = seq_index // blocks_per_tp
    column_start = (seq_index % blocks_per_tp) * column_width
    decode_hidden_cols = lax.dynamic_slice_in_dim(
        decode_hidden, column_start, column_width, axis=1
    ).astype(jnp.float32)
    last_hidden_cols = lax.dynamic_slice_in_dim(last_hidden, column_start, column_width, axis=1)
    head_hidden_cols = jnp.concatenate([decode_hidden_cols, last_hidden_cols], 0)
    head_attention = jnp.concatenate([decode_attention, last_attention], 0)
    head_part = jnp.dot(head_attention, out_weight, preferred_element_type=jnp.float32)
    head_part = jnp.where(owner_tp == tp_index, head_part + head_hidden_cols, head_part)
    head_all = lax.all_gather(head_part, ("seq", "tp"), axis=0)
    head_rows_count = decode_count + n_seq
    head_all = head_all.reshape(n_seq, n_tp, head_rows_count, column_width)
    head_sum = jnp.sum(head_all, axis=1)
    head_sum = jnp.transpose(head_sum, (1, 0, 2)).reshape(head_rows_count, model_width)
    head_updated = head_sum.astype(jnp.bfloat16)
    decode_out = lax.dynamic_slice_in_dim(
        head_updated[:decode_count], tp_index * feature_width, feature_width, axis=1
    )

    head_input = head_updated.astype(jnp.float32)
    mean_square = jnp.mean(head_input * head_input, axis=-1, keepdims=True)
    normed = (
        head_input * lax.rsqrt(mean_square + norm_eps) * final_gain.astype(jnp.float32)
    ).astype(jnp.bfloat16)
    logits = jnp.dot(normed, head_weight, preferred_element_type=jnp.float32)
    local_max = jnp.max(logits, axis=-1)
    local_sum = jnp.sum(jnp.exp(logits - local_max[:, None]), axis=-1)
    local_stats = jnp.stack([local_max, local_sum], -1)
    stats = doubling_gather(doubling_gather(local_stats, "tp"), "seq").reshape(
        (n_seq * n_tp,) + local_stats.shape
    )
    global_max = jnp.max(stats[..., 0], axis=0)
    global_sum = jnp.sum(stats[..., 1] * jnp.exp(stats[..., 0] - global_max[None]), axis=0)
    log_probs = logits - (global_max + jnp.log(global_sum))[:, None]
    every_row, decode_out, log_probs = lax.optimization_barrier((every_row, decode_out, log_probs))

    column_block = jnp.dot(every_row, out_weight, preferred_element_type=jnp.float32)
    prefill_block = column_block.reshape(n_seq, span_len, column_width)

    summed_rows = lax.psum_scatter(prefill_block, "tp", scatter_dimension=1, tiled=True)
    by_source = lax.all_to_all(summed_rows, "seq", split_axis=0, concat_axis=0, tiled=True)
    own_columns = lax.all_to_all(by_source, "tp", split_axis=0, concat_axis=1, tiled=True)
    projected = jnp.transpose(own_columns, (1, 0, 2)).reshape(span_len, feature_width)
    prefill_out = (prefill_hidden.astype(jnp.float32) + projected).astype(jnp.bfloat16)


    return (prefill_out, decode_out, log_probs)


def solution(mesh):
    return jax.shard_map(
        local,
        mesh=mesh,
        in_specs=(
            P("seq", "tp"),
            P("seq", "tp"),
            P(None, "seq", "tp"),
            P(None, "seq", None, "tp"),
            P(),
            P(None, "tp"),
            P(None, "tp"),
            P(None, None, "tp"),
            P(None, None, "seq", "tp"),
            P(),
            P(),
            P("tp", "seq"),
            P(),
            P(None, ("seq", "tp")),
        ),
        out_specs=(P("seq", "tp"), P(None, "tp"), P(None, ("seq", "tp"))),
        check_vma=False,
    )
```

```python
import math

import jax
import jax.numpy as jnp
from jax import lax
from jax.sharding import PartitionSpec as P

QUERY_HEADS = 40
KEY_HEADS = 8
HEAD_SIZE = 128


neg_large = -1e30
exact = lax.Precision.HIGHEST
norm_eps = 1e-06


def doubling_gather(value, axis):
    count = lax.axis_size(axis)
    if count & (count - 1):
        return lax.all_gather(value, axis, axis=0)
    index = lax.axis_index(axis)
    block = value[None]
    distance = 1
    while distance < count:
        pairs = [(i, i ^ distance) for i in range(count)]
        other = lax.ppermute(block, axis, pairs)
        low = (index & distance) == 0
        block = jnp.where(
            low, jnp.concatenate([block, other], 0), jnp.concatenate([other, block], 0)
        )
        distance *= 2
    return block


def local(
    prefill_hidden,
    prefill_query_rows,
    prefill_key_value,
    request_prefix_cache,
    prefix_lengths,
    decode_hidden,
    decode_query_rows,
    decode_kv,
    decode_slot_cache,
    cache_lengths,
    slot_table,
    out_weight,
    final_gain,
    head_weight,
):
    query_group_width = QUERY_HEADS // KEY_HEADS
    score_scale = 1.0 / math.sqrt(HEAD_SIZE)
    kv_local = prefill_key_value.shape[2] // HEAD_SIZE
    seq_index = lax.axis_index("seq")
    tp_index = lax.axis_index("tp")
    n_seq = lax.axis_size("seq")
    n_tp = lax.axis_size("tp")
    span_len = prefill_query_rows.shape[0]
    prefix_len = request_prefix_cache.shape[2]
    feature_width = prefill_hidden.shape[1]
    model_width = feature_width * n_tp
    column_width = out_weight.shape[1]
    decode_count = decode_query_rows.shape[0]

    ctx_local = decode_slot_cache.shape[2]
    chosen = jnp.take(decode_slot_cache, slot_table, axis=1)
    positions = seq_index * ctx_local + jnp.arange(ctx_local)
    decode_live = (positions[None, :] < cache_lengths[:, None])[:, None, None, :]
    decode_token_rows = decode_query_rows.reshape(
        decode_count, kv_local, query_group_width, HEAD_SIZE
    )
    cache_keys = chosen[0].reshape(decode_count, ctx_local, kv_local, HEAD_SIZE)
    cache_values = chosen[1].reshape(decode_count, ctx_local, kv_local, HEAD_SIZE)
    decode_scores = (
        jnp.einsum(
            "bkgh,bskh->bkgs", decode_token_rows, cache_keys, preferred_element_type=jnp.float32
        )
        * score_scale
    )
    decode_masked = jnp.where(decode_live, decode_scores, neg_large)
    decode_max = jnp.max(decode_masked, axis=-1).astype(jnp.bfloat16).astype(jnp.float32)
    decode_weights = jnp.where(decode_live, jnp.exp(decode_masked - decode_max[..., None]), 0.0)
    decode_sum = jnp.sum(decode_weights, axis=-1)
    decode_mixed = jnp.einsum(
        "bkgs,bskh->bkgh", decode_weights, cache_values.astype(jnp.float32), precision=exact
    )
    prefix_end = lax.dynamic_slice_in_dim(prefix_lengths, seq_index, 1)[0]
    query_matrix = prefill_query_rows.reshape(span_len, kv_local, query_group_width, HEAD_SIZE)
    joined_keys = jnp.concatenate([request_prefix_cache[0, 0], prefill_key_value[0]], 0).reshape(
        prefix_len + span_len, kv_local, HEAD_SIZE
    )
    value_matrix = jnp.concatenate([request_prefix_cache[1, 0], prefill_key_value[1]], 0).reshape(
        prefix_len + span_len, kv_local, HEAD_SIZE
    )
    key_place = jnp.arange(prefix_len + span_len)
    query_place = jnp.arange(span_len)
    live_mask = jnp.where(
        key_place[None, :] < prefix_len,
        key_place[None, :] < prefix_end,
        key_place[None, :] - prefix_len <= query_place[:, None],
    )
    scores = (
        jnp.einsum("rkgh,skh->kgrs", query_matrix, joined_keys, preferred_element_type=jnp.float32)
        * score_scale
    )
    masked = jnp.where(live_mask, scores, neg_large)
    row_max = jnp.max(masked, axis=-1, keepdims=True)
    weights = jnp.where(live_mask, jnp.exp(masked - row_max), 0.0)
    row_sum = jnp.sum(weights, axis=-1)
    weights_low = weights.astype(jnp.bfloat16)
    mixed = jnp.einsum(
        "kgrs,skh->rkgh", weights_low, value_matrix, preferred_element_type=jnp.float32
    )
    prefill_attention = (
        (mixed / jnp.transpose(row_sum, (2, 0, 1))[..., None])
        .astype(jnp.bfloat16)
        .reshape(span_len, -1)
    )
    sum_high = decode_sum.astype(jnp.bfloat16)
    sum_low = (decode_sum - sum_high.astype(jnp.float32)).astype(jnp.bfloat16)
    mixed_high = decode_mixed.astype(jnp.bfloat16)
    mixed_low = (decode_mixed - mixed_high.astype(jnp.float32)).astype(jnp.bfloat16)
    stat_count = decode_sum.size
    decode_flat = jnp.concatenate(
        [
            decode_max.astype(jnp.bfloat16).reshape(-1),
            sum_high.reshape(-1),
            sum_low.reshape(-1),
            mixed_high.reshape(-1),
            mixed_low.reshape(-1),
        ]
    )
    extra_rows = -(-decode_flat.size // feature_width)
    decode_flat = jnp.pad(decode_flat, (0, extra_rows * feature_width - decode_flat.size))
    small_rows = jnp.concatenate(
        [
            prefill_attention[span_len - 1 :],
            prefill_hidden[span_len - 1 :],
            decode_flat.reshape(extra_rows, feature_width),
        ],
        0,
    )
    small_gathered = lax.all_gather(small_rows, "seq", axis=0)
    every_row = lax.all_gather(prefill_attention, "seq", axis=0).reshape(n_seq * span_len, feature_width)
    last_attention = small_gathered[:, 0]
    last_hidden = small_gathered[:, 1].astype(jnp.float32)
    every_flat = small_gathered[:, 2:].reshape(n_seq, -1).astype(jnp.float32)
    mixed_count = decode_mixed.size
    part_max = every_flat[:, :stat_count].reshape((n_seq,) + decode_sum.shape)
    part_sum = (
        every_flat[:, stat_count : 2 * stat_count] + every_flat[:, 2 * stat_count : 3 * stat_count]
    ).reshape((n_seq,) + decode_sum.shape)
    mixed_at = 3 * stat_count
    part_mixed = (
        every_flat[:, mixed_at : mixed_at + mixed_count]
        + every_flat[:, mixed_at + mixed_count : mixed_at + 2 * mixed_count]
    ).reshape((n_seq,) + decode_mixed.shape)

    best = jnp.max(part_max, axis=0)
    factors = jnp.exp(part_max - best[None])
    totals = jnp.sum(part_sum * factors, axis=0)
    mixtures = jnp.sum(part_mixed * factors[..., None], axis=0)
    own_keys = decode_kv[0].reshape(decode_count, kv_local, HEAD_SIZE)
    own_values = decode_kv[1].reshape(decode_count, kv_local, HEAD_SIZE).astype(jnp.float32)
    own_scores = (
        jnp.einsum("bkgh,bkh->bkg", decode_token_rows, own_keys, preferred_element_type=jnp.float32)
        * score_scale
    )
    final_max = jnp.maximum(best, own_scores)
    factor_one = jnp.exp(best - final_max)
    factor_two = jnp.exp(own_scores - final_max)
    final_sum = totals * factor_one + factor_two
    final_mixed = mixtures * factor_one[..., None] + own_values[:, :, None, :] * factor_two[..., None]
    decode_attention = (
        (final_mixed / final_sum[..., None]).astype(jnp.bfloat16).reshape(decode_count, -1)
    )

    blocks_per_tp = n_seq // n_tp
    owner_tp = seq_index // blocks_per_tp
    column_start = (seq_index % blocks_per_tp) * column_width
    decode_hidden_cols = lax.dynamic_slice_in_dim(
        decode_hidden, column_start, column_width, axis=1
    ).astype(jnp.float32)
    last_hidden_cols = lax.dynamic_slice_in_dim(last_hidden, column_start, column_width, axis=1)
    head_hidden_cols = jnp.concatenate([decode_hidden_cols, last_hidden_cols], 0)
    head_attention = jnp.concatenate([decode_attention, last_attention], 0)
    head_part = jnp.dot(head_attention, out_weight, preferred_element_type=jnp.float32)
    head_part = jnp.where(owner_tp == tp_index, head_part + head_hidden_cols, head_part)
    head_all = lax.all_gather(head_part, ("seq", "tp"), axis=0)
    head_rows_count = decode_count + n_seq
    head_all = head_all.reshape(n_seq, n_tp, head_rows_count, column_width)
    head_sum = jnp.sum(head_all, axis=1)
    head_sum = jnp.transpose(head_sum, (1, 0, 2)).reshape(head_rows_count, model_width)
    head_updated = head_sum.astype(jnp.bfloat16)
    decode_out = lax.dynamic_slice_in_dim(
        head_updated[:decode_count], tp_index * feature_width, feature_width, axis=1
    )

    head_input = head_updated.astype(jnp.float32)
    mean_square = jnp.mean(head_input * head_input, axis=-1, keepdims=True)
    normed = (
        head_input * lax.rsqrt(mean_square + norm_eps) * final_gain.astype(jnp.float32)
    ).astype(jnp.bfloat16)
    logits = jnp.dot(normed, head_weight, preferred_element_type=jnp.float32)
    local_max = jnp.max(logits, axis=-1)
    local_sum = jnp.sum(jnp.exp(logits - local_max[:, None]), axis=-1)
    local_stats = jnp.stack([local_max, local_sum], -1)
    every_row, local_stats = lax.optimization_barrier((every_row, local_stats))
    stats = doubling_gather(doubling_gather(local_stats, "tp"), "seq").reshape(
        (n_seq * n_tp,) + local_stats.shape
    )
    global_max = jnp.max(stats[..., 0], axis=0)
    global_sum = jnp.sum(stats[..., 1] * jnp.exp(stats[..., 0] - global_max[None]), axis=0)
    log_probs = logits - (global_max + jnp.log(global_sum))[:, None]

    column_block = jnp.dot(every_row, out_weight, preferred_element_type=jnp.float32)
    prefill_block = column_block.reshape(n_seq, span_len, column_width)

    summed_rows = lax.psum_scatter(prefill_block, "tp", scatter_dimension=1, tiled=True)
    by_source = lax.all_to_all(summed_rows, "seq", split_axis=0, concat_axis=0, tiled=True)
    own_columns = lax.all_to_all(by_source, "tp", split_axis=0, concat_axis=1, tiled=True)
    projected = jnp.transpose(own_columns, (1, 0, 2)).reshape(span_len, feature_width)
    prefill_out = (prefill_hidden.astype(jnp.float32) + projected).astype(jnp.bfloat16)


    return (prefill_out, decode_out, log_probs)


def solution(mesh):
    return jax.shard_map(
        local,
        mesh=mesh,
        in_specs=(
            P("seq", "tp"),
            P("seq", "tp"),
            P(None, "seq", "tp"),
            P(None, "seq", None, "tp"),
            P(),
            P(None, "tp"),
            P(None, "tp"),
            P(None, None, "tp"),
            P(None, None, "seq", "tp"),
            P(),
            P(),
            P("tp", "seq"),
            P(),
            P(None, ("seq", "tp")),
        ),
        out_specs=(P("seq", "tp"), P(None, "tp"), P(None, ("seq", "tp"))),
        check_vma=False,
    )
```

```python
import math

import jax
import jax.numpy as jnp
from jax import lax
from jax.sharding import PartitionSpec as P

QUERY_HEADS = 40
KEY_HEADS = 8
HEAD_SIZE = 128


neg_large = -1e30
exact = lax.Precision.HIGHEST
norm_eps = 1e-06


def doubling_gather(value, axis):
    count = lax.axis_size(axis)
    if count & (count - 1):
        return lax.all_gather(value, axis, axis=0)
    index = lax.axis_index(axis)
    block = value[None]
    steps = 0
    distance = count // 2
    while distance >= 1:
        pairs = [(i, i ^ distance) for i in range(count)]
        other = lax.ppermute(block, axis, pairs)
        low = (index & distance) == 0
        block = jnp.where(
            low, jnp.concatenate([block, other], 0), jnp.concatenate([other, block], 0)
        )
        steps += 1
        distance //= 2
    rest = value.shape
    block = block.reshape((2,) * steps + rest)
    order = tuple(range(steps - 1, -1, -1)) + tuple(range(steps, steps + len(rest)))
    return jnp.transpose(block, order).reshape((count,) + rest)


def local(
    prefill_hidden,
    prefill_query_rows,
    prefill_key_value,
    request_prefix_cache,
    prefix_lengths,
    decode_hidden,
    decode_query_rows,
    decode_kv,
    decode_slot_cache,
    cache_lengths,
    slot_table,
    out_weight,
    final_gain,
    head_weight,
):
    query_group_width = QUERY_HEADS // KEY_HEADS
    score_scale = 1.0 / math.sqrt(HEAD_SIZE)
    kv_local = prefill_key_value.shape[2] // HEAD_SIZE
    seq_index = lax.axis_index("seq")
    tp_index = lax.axis_index("tp")
    n_seq = lax.axis_size("seq")
    n_tp = lax.axis_size("tp")
    span_len = prefill_query_rows.shape[0]
    prefix_len = request_prefix_cache.shape[2]
    feature_width = prefill_hidden.shape[1]
    model_width = feature_width * n_tp
    column_width = out_weight.shape[1]
    decode_count = decode_query_rows.shape[0]

    ctx_local = decode_slot_cache.shape[2]
    chosen = jnp.take(decode_slot_cache, slot_table, axis=1)
    positions = seq_index * ctx_local + jnp.arange(ctx_local)
    decode_live = (positions[None, :] < cache_lengths[:, None])[:, None, None, :]
    decode_token_rows = decode_query_rows.reshape(
        decode_count, kv_local, query_group_width, HEAD_SIZE
    )
    cache_keys = chosen[0].reshape(decode_count, ctx_local, kv_local, HEAD_SIZE)
    cache_values = chosen[1].reshape(decode_count, ctx_local, kv_local, HEAD_SIZE)
    decode_scores = (
        jnp.einsum(
            "bkgh,bskh->bkgs", decode_token_rows, cache_keys, preferred_element_type=jnp.float32
        )
        * score_scale
    )
    decode_masked = jnp.where(decode_live, decode_scores, neg_large)
    decode_max = jnp.max(decode_masked, axis=-1).astype(jnp.bfloat16).astype(jnp.float32)
    decode_weights = jnp.where(decode_live, jnp.exp(decode_masked - decode_max[..., None]), 0.0)
    decode_sum = jnp.sum(decode_weights, axis=-1)
    decode_mixed = jnp.einsum(
        "bkgs,bskh->bkgh", decode_weights, cache_values.astype(jnp.float32), precision=exact
    )
    prefix_end = lax.dynamic_slice_in_dim(prefix_lengths, seq_index, 1)[0]
    query_matrix = prefill_query_rows.reshape(span_len, kv_local, query_group_width, HEAD_SIZE)
    joined_keys = jnp.concatenate([request_prefix_cache[0, 0], prefill_key_value[0]], 0).reshape(
        prefix_len + span_len, kv_local, HEAD_SIZE
    )
    value_matrix = jnp.concatenate([request_prefix_cache[1, 0], prefill_key_value[1]], 0).reshape(
        prefix_len + span_len, kv_local, HEAD_SIZE
    )
    key_place = jnp.arange(prefix_len + span_len)
    query_place = jnp.arange(span_len)
    live_mask = jnp.where(
        key_place[None, :] < prefix_len,
        key_place[None, :] < prefix_end,
        key_place[None, :] - prefix_len <= query_place[:, None],
    )
    scores = (
        jnp.einsum("rkgh,skh->kgrs", query_matrix, joined_keys, preferred_element_type=jnp.float32)
        * score_scale
    )
    masked = jnp.where(live_mask, scores, neg_large)
    row_max = jnp.max(masked, axis=-1, keepdims=True)
    weights = jnp.where(live_mask, jnp.exp(masked - row_max), 0.0)
    row_sum = jnp.sum(weights, axis=-1)
    weights_low = weights.astype(jnp.bfloat16)
    mixed = jnp.einsum(
        "kgrs,skh->rkgh", weights_low, value_matrix, preferred_element_type=jnp.float32
    )
    prefill_attention = (
        (mixed / jnp.transpose(row_sum, (2, 0, 1))[..., None])
        .astype(jnp.bfloat16)
        .reshape(span_len, -1)
    )
    sum_high = decode_sum.astype(jnp.bfloat16)
    sum_low = (decode_sum - sum_high.astype(jnp.float32)).astype(jnp.bfloat16)
    mixed_high = decode_mixed.astype(jnp.bfloat16)
    mixed_low = (decode_mixed - mixed_high.astype(jnp.float32)).astype(jnp.bfloat16)
    stat_count = decode_sum.size
    decode_flat = jnp.concatenate(
        [
            decode_max.astype(jnp.bfloat16).reshape(-1),
            sum_high.reshape(-1),
            sum_low.reshape(-1),
            mixed_high.reshape(-1),
            mixed_low.reshape(-1),
        ]
    )
    extra_rows = -(-decode_flat.size // feature_width)
    decode_flat = jnp.pad(decode_flat, (0, extra_rows * feature_width - decode_flat.size))
    small_rows = jnp.concatenate(
        [
            prefill_attention[span_len - 1 :],
            prefill_hidden[span_len - 1 :],
            decode_flat.reshape(extra_rows, feature_width),
        ],
        0,
    )
    small_gathered = doubling_gather(small_rows, "seq")
    every_row = lax.all_gather(prefill_attention, "seq", axis=0).reshape(n_seq * span_len, feature_width)
    last_attention = small_gathered[:, 0]
    last_hidden = small_gathered[:, 1].astype(jnp.float32)
    every_flat = small_gathered[:, 2:].reshape(n_seq, -1).astype(jnp.float32)
    mixed_count = decode_mixed.size
    part_max = every_flat[:, :stat_count].reshape((n_seq,) + decode_sum.shape)
    part_sum = (
        every_flat[:, stat_count : 2 * stat_count] + every_flat[:, 2 * stat_count : 3 * stat_count]
    ).reshape((n_seq,) + decode_sum.shape)
    mixed_at = 3 * stat_count
    part_mixed = (
        every_flat[:, mixed_at : mixed_at + mixed_count]
        + every_flat[:, mixed_at + mixed_count : mixed_at + 2 * mixed_count]
    ).reshape((n_seq,) + decode_mixed.shape)

    best = jnp.max(part_max, axis=0)
    factors = jnp.exp(part_max - best[None])
    totals = jnp.sum(part_sum * factors, axis=0)
    mixtures = jnp.sum(part_mixed * factors[..., None], axis=0)
    own_keys = decode_kv[0].reshape(decode_count, kv_local, HEAD_SIZE)
    own_values = decode_kv[1].reshape(decode_count, kv_local, HEAD_SIZE).astype(jnp.float32)
    own_scores = (
        jnp.einsum("bkgh,bkh->bkg", decode_token_rows, own_keys, preferred_element_type=jnp.float32)
        * score_scale
    )
    final_max = jnp.maximum(best, own_scores)
    factor_one = jnp.exp(best - final_max)
    factor_two = jnp.exp(own_scores - final_max)
    final_sum = totals * factor_one + factor_two
    final_mixed = mixtures * factor_one[..., None] + own_values[:, :, None, :] * factor_two[..., None]
    decode_attention = (
        (final_mixed / final_sum[..., None]).astype(jnp.bfloat16).reshape(decode_count, -1)
    )

    blocks_per_tp = n_seq // n_tp
    owner_tp = seq_index // blocks_per_tp
    column_start = (seq_index % blocks_per_tp) * column_width
    decode_hidden_cols = lax.dynamic_slice_in_dim(
        decode_hidden, column_start, column_width, axis=1
    ).astype(jnp.float32)
    last_hidden_cols = lax.dynamic_slice_in_dim(last_hidden, column_start, column_width, axis=1)
    head_hidden_cols = jnp.concatenate([decode_hidden_cols, last_hidden_cols], 0)
    head_attention = jnp.concatenate([decode_attention, last_attention], 0)
    head_part = jnp.dot(head_attention, out_weight, preferred_element_type=jnp.float32)
    head_part = jnp.where(owner_tp == tp_index, head_part + head_hidden_cols, head_part)
    head_all = doubling_gather(doubling_gather(head_part, "tp"), "seq")
    head_rows_count = decode_count + n_seq
    head_all = head_all.reshape(n_seq, n_tp, head_rows_count, column_width)
    head_sum = jnp.sum(head_all, axis=1)
    head_sum = jnp.transpose(head_sum, (1, 0, 2)).reshape(head_rows_count, model_width)
    head_updated = head_sum.astype(jnp.bfloat16)
    decode_out = lax.dynamic_slice_in_dim(
        head_updated[:decode_count], tp_index * feature_width, feature_width, axis=1
    )

    head_input = head_updated.astype(jnp.float32)
    mean_square = jnp.mean(head_input * head_input, axis=-1, keepdims=True)
    normed = (
        head_input * lax.rsqrt(mean_square + norm_eps) * final_gain.astype(jnp.float32)
    ).astype(jnp.bfloat16)
    logits = jnp.dot(normed, head_weight, preferred_element_type=jnp.float32)
    local_max = jnp.max(logits, axis=-1)
    local_sum = jnp.sum(jnp.exp(logits - local_max[:, None]), axis=-1)
    local_stats = jnp.stack([local_max, local_sum], -1)
    every_row, local_stats = lax.optimization_barrier((every_row, local_stats))
    stats = doubling_gather(doubling_gather(local_stats, "tp"), "seq").reshape(
        (n_seq * n_tp,) + local_stats.shape
    )
    global_max = jnp.max(stats[..., 0], axis=0)
    global_sum = jnp.sum(stats[..., 1] * jnp.exp(stats[..., 0] - global_max[None]), axis=0)
    log_probs = logits - (global_max + jnp.log(global_sum))[:, None]

    column_block = jnp.dot(every_row, out_weight, preferred_element_type=jnp.float32)
    prefill_block = column_block.reshape(n_seq, span_len, column_width)

    summed_rows = lax.psum_scatter(prefill_block, "tp", scatter_dimension=1, tiled=True)
    by_source = lax.all_to_all(summed_rows, "seq", split_axis=0, concat_axis=0, tiled=True)
    own_columns = lax.all_to_all(by_source, "tp", split_axis=0, concat_axis=1, tiled=True)
    projected = jnp.transpose(own_columns, (1, 0, 2)).reshape(span_len, feature_width)
    prefill_out = (prefill_hidden.astype(jnp.float32) + projected).astype(jnp.bfloat16)


    return (prefill_out, decode_out, log_probs)


def solution(mesh):
    return jax.shard_map(
        local,
        mesh=mesh,
        in_specs=(
            P("seq", "tp"),
            P("seq", "tp"),
            P(None, "seq", "tp"),
            P(None, "seq", None, "tp"),
            P(),
            P(None, "tp"),
            P(None, "tp"),
            P(None, None, "tp"),
            P(None, None, "seq", "tp"),
            P(),
            P(),
            P("tp", "seq"),
            P(),
            P(None, ("seq", "tp")),
        ),
        out_specs=(P("seq", "tp"), P(None, "tp"), P(None, ("seq", "tp"))),
        check_vma=False,
    )
```

```python
import math

import jax
import jax.numpy as jnp
from jax import lax
from jax.sharding import PartitionSpec as P

QUERY_HEADS = 40
KEY_HEADS = 8
HEAD_SIZE = 128


neg_large = -1e30
exact = lax.Precision.HIGHEST
norm_eps = 1e-06


def doubling_gather(value, axis, high_first=False):
    count = lax.axis_size(axis)
    if count & (count - 1):
        return lax.all_gather(value, axis, axis=0)
    index = lax.axis_index(axis)
    block = value[None]
    distances = []
    distance = 1
    while distance < count:
        distances.append(distance)
        distance *= 2
    if high_first:
        distances = distances[::-1]
    for distance in distances:
        pairs = [(i, i ^ distance) for i in range(count)]
        other = lax.ppermute(block, axis, pairs)
        low = (index & distance) == 0
        block = jnp.where(
            low, jnp.concatenate([block, other], 0), jnp.concatenate([other, block], 0)
        )
    if not high_first:
        return block
    steps = len(distances)
    rest = value.shape
    block = block.reshape((2,) * steps + rest)
    order = tuple(range(steps - 1, -1, -1)) + tuple(range(steps, steps + len(rest)))
    return jnp.transpose(block, order).reshape((count,) + rest)


def local(
    prefill_hidden,
    prefill_query_rows,
    prefill_key_value,
    request_prefix_cache,
    prefix_lengths,
    decode_hidden,
    decode_query_rows,
    decode_kv,
    decode_slot_cache,
    cache_lengths,
    slot_table,
    out_weight,
    final_gain,
    head_weight,
):
    query_group_width = QUERY_HEADS // KEY_HEADS
    score_scale = 1.0 / math.sqrt(HEAD_SIZE)
    kv_local = prefill_key_value.shape[2] // HEAD_SIZE
    seq_index = lax.axis_index("seq")
    tp_index = lax.axis_index("tp")
    n_seq = lax.axis_size("seq")
    n_tp = lax.axis_size("tp")
    span_len = prefill_query_rows.shape[0]
    prefix_len = request_prefix_cache.shape[2]
    feature_width = prefill_hidden.shape[1]
    model_width = feature_width * n_tp
    column_width = out_weight.shape[1]
    decode_count = decode_query_rows.shape[0]

    ctx_local = decode_slot_cache.shape[2]
    chosen = jnp.take(decode_slot_cache, slot_table, axis=1)
    positions = seq_index * ctx_local + jnp.arange(ctx_local)
    decode_live = (positions[None, :] < cache_lengths[:, None])[:, None, None, :]
    decode_token_rows = decode_query_rows.reshape(
        decode_count, kv_local, query_group_width, HEAD_SIZE
    )
    cache_keys = chosen[0].reshape(decode_count, ctx_local, kv_local, HEAD_SIZE)
    cache_values = chosen[1].reshape(decode_count, ctx_local, kv_local, HEAD_SIZE)
    decode_scores = (
        jnp.einsum(
            "bkgh,bskh->bkgs", decode_token_rows, cache_keys, preferred_element_type=jnp.float32
        )
        * score_scale
    )
    decode_masked = jnp.where(decode_live, decode_scores, neg_large)
    decode_max = jnp.max(decode_masked, axis=-1).astype(jnp.bfloat16).astype(jnp.float32)
    decode_weights = jnp.where(decode_live, jnp.exp(decode_masked - decode_max[..., None]), 0.0)
    decode_sum = jnp.sum(decode_weights, axis=-1)
    decode_mixed = jnp.einsum(
        "bkgs,bskh->bkgh", decode_weights, cache_values.astype(jnp.float32), precision=exact
    )
    prefix_end = lax.dynamic_slice_in_dim(prefix_lengths, seq_index, 1)[0]
    query_matrix = prefill_query_rows.reshape(span_len, kv_local, query_group_width, HEAD_SIZE)
    joined_keys = jnp.concatenate([request_prefix_cache[0, 0], prefill_key_value[0]], 0).reshape(
        prefix_len + span_len, kv_local, HEAD_SIZE
    )
    value_matrix = jnp.concatenate([request_prefix_cache[1, 0], prefill_key_value[1]], 0).reshape(
        prefix_len + span_len, kv_local, HEAD_SIZE
    )
    key_place = jnp.arange(prefix_len + span_len)
    query_place = jnp.arange(span_len)
    live_mask = jnp.where(
        key_place[None, :] < prefix_len,
        key_place[None, :] < prefix_end,
        key_place[None, :] - prefix_len <= query_place[:, None],
    )
    scores = (
        jnp.einsum("rkgh,skh->kgrs", query_matrix, joined_keys, preferred_element_type=jnp.float32)
        * score_scale
    )
    masked = jnp.where(live_mask, scores, neg_large)
    row_max = jnp.max(masked, axis=-1, keepdims=True)
    weights = jnp.where(live_mask, jnp.exp(masked - row_max), 0.0)
    row_sum = jnp.sum(weights, axis=-1)
    weights_low = weights.astype(jnp.bfloat16)
    mixed = jnp.einsum(
        "kgrs,skh->rkgh", weights_low, value_matrix, preferred_element_type=jnp.float32
    )
    prefill_attention = (
        (mixed / jnp.transpose(row_sum, (2, 0, 1))[..., None])
        .astype(jnp.bfloat16)
        .reshape(span_len, -1)
    )
    sum_high = decode_sum.astype(jnp.bfloat16)
    sum_low = (decode_sum - sum_high.astype(jnp.float32)).astype(jnp.bfloat16)
    mixed_high = decode_mixed.astype(jnp.bfloat16)
    mixed_low = (decode_mixed - mixed_high.astype(jnp.float32)).astype(jnp.bfloat16)
    stat_count = decode_sum.size
    decode_flat = jnp.concatenate(
        [
            decode_max.astype(jnp.bfloat16).reshape(-1),
            sum_high.reshape(-1),
            sum_low.reshape(-1),
            mixed_high.reshape(-1),
            mixed_low.reshape(-1),
        ]
    )
    extra_rows = -(-decode_flat.size // feature_width)
    decode_flat = jnp.pad(decode_flat, (0, extra_rows * feature_width - decode_flat.size))
    small_rows = jnp.concatenate(
        [
            prefill_attention[span_len - 1 :],
            prefill_hidden[span_len - 1 :],
            decode_flat.reshape(extra_rows, feature_width),
        ],
        0,
    )
    small_gathered = doubling_gather(small_rows, "seq", high_first=True)
    every_row = lax.all_gather(prefill_attention, "seq", axis=0).reshape(n_seq * span_len, feature_width)
    last_attention = small_gathered[:, 0]
    last_hidden = small_gathered[:, 1].astype(jnp.float32)
    every_flat = small_gathered[:, 2:].reshape(n_seq, -1).astype(jnp.float32)
    mixed_count = decode_mixed.size
    part_max = every_flat[:, :stat_count].reshape((n_seq,) + decode_sum.shape)
    part_sum = (
        every_flat[:, stat_count : 2 * stat_count] + every_flat[:, 2 * stat_count : 3 * stat_count]
    ).reshape((n_seq,) + decode_sum.shape)
    mixed_at = 3 * stat_count
    part_mixed = (
        every_flat[:, mixed_at : mixed_at + mixed_count]
        + every_flat[:, mixed_at + mixed_count : mixed_at + 2 * mixed_count]
    ).reshape((n_seq,) + decode_mixed.shape)

    best = jnp.max(part_max, axis=0)
    factors = jnp.exp(part_max - best[None])
    totals = jnp.sum(part_sum * factors, axis=0)
    mixtures = jnp.sum(part_mixed * factors[..., None], axis=0)
    own_keys = decode_kv[0].reshape(decode_count, kv_local, HEAD_SIZE)
    own_values = decode_kv[1].reshape(decode_count, kv_local, HEAD_SIZE).astype(jnp.float32)
    own_scores = (
        jnp.einsum("bkgh,bkh->bkg", decode_token_rows, own_keys, preferred_element_type=jnp.float32)
        * score_scale
    )
    final_max = jnp.maximum(best, own_scores)
    factor_one = jnp.exp(best - final_max)
    factor_two = jnp.exp(own_scores - final_max)
    final_sum = totals * factor_one + factor_two
    final_mixed = mixtures * factor_one[..., None] + own_values[:, :, None, :] * factor_two[..., None]
    decode_attention = (
        (final_mixed / final_sum[..., None]).astype(jnp.bfloat16).reshape(decode_count, -1)
    )

    blocks_per_tp = n_seq // n_tp
    owner_tp = seq_index // blocks_per_tp
    column_start = (seq_index % blocks_per_tp) * column_width
    decode_hidden_cols = lax.dynamic_slice_in_dim(
        decode_hidden, column_start, column_width, axis=1
    ).astype(jnp.float32)
    last_hidden_cols = lax.dynamic_slice_in_dim(last_hidden, column_start, column_width, axis=1)
    head_hidden_cols = jnp.concatenate([decode_hidden_cols, last_hidden_cols], 0)
    head_attention = jnp.concatenate([decode_attention, last_attention], 0)
    head_part = jnp.dot(head_attention, out_weight, preferred_element_type=jnp.float32)
    head_part = jnp.where(owner_tp == tp_index, head_part + head_hidden_cols, head_part)
    head_all = lax.all_gather(head_part, ("seq", "tp"), axis=0)
    head_rows_count = decode_count + n_seq
    head_all = head_all.reshape(n_seq, n_tp, head_rows_count, column_width)
    head_sum = jnp.sum(head_all, axis=1)
    head_sum = jnp.transpose(head_sum, (1, 0, 2)).reshape(head_rows_count, model_width)
    head_updated = head_sum.astype(jnp.bfloat16)
    decode_out = lax.dynamic_slice_in_dim(
        head_updated[:decode_count], tp_index * feature_width, feature_width, axis=1
    )

    head_input = head_updated.astype(jnp.float32)
    mean_square = jnp.mean(head_input * head_input, axis=-1, keepdims=True)
    normed = (
        head_input * lax.rsqrt(mean_square + norm_eps) * final_gain.astype(jnp.float32)
    ).astype(jnp.bfloat16)
    logits = jnp.dot(normed, head_weight, preferred_element_type=jnp.float32)
    local_max = jnp.max(logits, axis=-1)
    local_sum = jnp.sum(jnp.exp(logits - local_max[:, None]), axis=-1)
    local_stats = jnp.stack([local_max, local_sum], -1)
    every_row, local_stats = lax.optimization_barrier((every_row, local_stats))
    stats = doubling_gather(doubling_gather(local_stats, "tp"), "seq").reshape(
        (n_seq * n_tp,) + local_stats.shape
    )
    global_max = jnp.max(stats[..., 0], axis=0)
    global_sum = jnp.sum(stats[..., 1] * jnp.exp(stats[..., 0] - global_max[None]), axis=0)
    log_probs = logits - (global_max + jnp.log(global_sum))[:, None]

    column_block = jnp.dot(every_row, out_weight, preferred_element_type=jnp.float32)
    prefill_block = column_block.reshape(n_seq, span_len, column_width)

    summed_rows = lax.psum_scatter(prefill_block, "tp", scatter_dimension=1, tiled=True)
    by_source = lax.all_to_all(summed_rows, "seq", split_axis=0, concat_axis=0, tiled=True)
    own_columns = lax.all_to_all(by_source, "tp", split_axis=0, concat_axis=1, tiled=True)
    projected = jnp.transpose(own_columns, (1, 0, 2)).reshape(span_len, feature_width)
    prefill_out = (prefill_hidden.astype(jnp.float32) + projected).astype(jnp.bfloat16)


    return (prefill_out, decode_out, log_probs)


def solution(mesh):
    return jax.shard_map(
        local,
        mesh=mesh,
        in_specs=(
            P("seq", "tp"),
            P("seq", "tp"),
            P(None, "seq", "tp"),
            P(None, "seq", None, "tp"),
            P(),
            P(None, "tp"),
            P(None, "tp"),
            P(None, None, "tp"),
            P(None, None, "seq", "tp"),
            P(),
            P(),
            P("tp", "seq"),
            P(),
            P(None, ("seq", "tp")),
        ),
        out_specs=(P("seq", "tp"), P(None, "tp"), P(None, ("seq", "tp"))),
        check_vma=False,
    )
```

```python
import math

import jax
import jax.numpy as jnp
from jax import lax
from jax.sharding import PartitionSpec as P

QUERY_HEADS = 40
KEY_HEADS = 8
HEAD_SIZE = 128


neg_large = -1e30
exact = lax.Precision.HIGHEST
norm_eps = 1e-06


def doubling_gather(value, axis, high_first=False):
    count = lax.axis_size(axis)
    if count & (count - 1):
        return lax.all_gather(value, axis, axis=0)
    index = lax.axis_index(axis)
    block = value[None]
    distances = []
    distance = 1
    while distance < count:
        distances.append(distance)
        distance *= 2
    if high_first:
        distances = distances[::-1]
    for distance in distances:
        pairs = [(i, i ^ distance) for i in range(count)]
        other = lax.ppermute(block, axis, pairs)
        low = (index & distance) == 0
        block = jnp.where(
            low, jnp.concatenate([block, other], 0), jnp.concatenate([other, block], 0)
        )
    if not high_first:
        return block
    steps = len(distances)
    rest = value.shape
    block = block.reshape((2,) * steps + rest)
    order = tuple(range(steps - 1, -1, -1)) + tuple(range(steps, steps + len(rest)))
    return jnp.transpose(block, order).reshape((count,) + rest)


def local(
    prefill_hidden,
    prefill_query_rows,
    prefill_key_value,
    request_prefix_cache,
    prefix_lengths,
    decode_hidden,
    decode_query_rows,
    decode_kv,
    decode_slot_cache,
    cache_lengths,
    slot_table,
    out_weight,
    final_gain,
    head_weight,
):
    query_group_width = QUERY_HEADS // KEY_HEADS
    score_scale = 1.0 / math.sqrt(HEAD_SIZE)
    kv_local = prefill_key_value.shape[2] // HEAD_SIZE
    seq_index = lax.axis_index("seq")
    tp_index = lax.axis_index("tp")
    n_seq = lax.axis_size("seq")
    n_tp = lax.axis_size("tp")
    span_len = prefill_query_rows.shape[0]
    prefix_len = request_prefix_cache.shape[2]
    feature_width = prefill_hidden.shape[1]
    model_width = feature_width * n_tp
    column_width = out_weight.shape[1]
    decode_count = decode_query_rows.shape[0]

    ctx_local = decode_slot_cache.shape[2]
    chosen = jnp.take(decode_slot_cache, slot_table, axis=1)
    positions = seq_index * ctx_local + jnp.arange(ctx_local)
    decode_live = (positions[None, :] < cache_lengths[:, None])[:, None, None, :]
    decode_token_rows = decode_query_rows.reshape(
        decode_count, kv_local, query_group_width, HEAD_SIZE
    )
    cache_keys = chosen[0].reshape(decode_count, ctx_local, kv_local, HEAD_SIZE)
    cache_values = chosen[1].reshape(decode_count, ctx_local, kv_local, HEAD_SIZE)
    decode_scores = (
        jnp.einsum(
            "bkgh,bskh->bkgs", decode_token_rows, cache_keys, preferred_element_type=jnp.float32
        )
        * score_scale
    )
    decode_masked = jnp.where(decode_live, decode_scores, neg_large)
    decode_max = jnp.max(decode_masked, axis=-1).astype(jnp.bfloat16).astype(jnp.float32)
    decode_weights = jnp.where(decode_live, jnp.exp(decode_masked - decode_max[..., None]), 0.0)
    decode_sum = jnp.sum(decode_weights, axis=-1)
    decode_mixed = jnp.einsum(
        "bkgs,bskh->bkgh", decode_weights, cache_values.astype(jnp.float32), precision=exact
    )
    prefix_end = lax.dynamic_slice_in_dim(prefix_lengths, seq_index, 1)[0]
    query_matrix = prefill_query_rows.reshape(span_len, kv_local, query_group_width, HEAD_SIZE)
    joined_keys = jnp.concatenate([request_prefix_cache[0, 0], prefill_key_value[0]], 0).reshape(
        prefix_len + span_len, kv_local, HEAD_SIZE
    )
    value_matrix = jnp.concatenate([request_prefix_cache[1, 0], prefill_key_value[1]], 0).reshape(
        prefix_len + span_len, kv_local, HEAD_SIZE
    )
    key_place = jnp.arange(prefix_len + span_len)
    query_place = jnp.arange(span_len)
    live_mask = jnp.where(
        key_place[None, :] < prefix_len,
        key_place[None, :] < prefix_end,
        key_place[None, :] - prefix_len <= query_place[:, None],
    )
    scores = (
        jnp.einsum("rkgh,skh->kgrs", query_matrix, joined_keys, preferred_element_type=jnp.float32)
        * score_scale
    )
    masked = jnp.where(live_mask, scores, neg_large)
    row_max = jnp.max(masked, axis=-1, keepdims=True)
    weights = jnp.where(live_mask, jnp.exp(masked - row_max), 0.0)
    row_sum = jnp.sum(weights, axis=-1)
    weights_low = weights.astype(jnp.bfloat16)
    mixed = jnp.einsum(
        "kgrs,skh->rkgh", weights_low, value_matrix, preferred_element_type=jnp.float32
    )
    prefill_attention = (
        (mixed / jnp.transpose(row_sum, (2, 0, 1))[..., None])
        .astype(jnp.bfloat16)
        .reshape(span_len, -1)
    )
    sum_high = decode_sum.astype(jnp.bfloat16)
    sum_low = (decode_sum - sum_high.astype(jnp.float32)).astype(jnp.bfloat16)
    mixed_high = decode_mixed.astype(jnp.bfloat16)
    mixed_low = (decode_mixed - mixed_high.astype(jnp.float32)).astype(jnp.bfloat16)
    stat_count = decode_sum.size
    decode_flat = jnp.concatenate(
        [
            decode_max.astype(jnp.bfloat16).reshape(-1),
            sum_high.reshape(-1),
            sum_low.reshape(-1),
            mixed_high.reshape(-1),
            mixed_low.reshape(-1),
        ]
    )
    extra_rows = -(-decode_flat.size // feature_width)
    decode_flat = jnp.pad(decode_flat, (0, extra_rows * feature_width - decode_flat.size))
    small_rows = jnp.concatenate(
        [
            prefill_attention[span_len - 1 :],
            prefill_hidden[span_len - 1 :],
            decode_flat.reshape(extra_rows, feature_width),
        ],
        0,
    )
    small_gathered = doubling_gather(small_rows, "seq", high_first=True)
    chunk_rows = span_len // 2
    every_chunk = [
        lax.all_gather(prefill_attention[c * chunk_rows : (c + 1) * chunk_rows], "seq", axis=0)
        for c in range(2)
    ]
    last_attention = small_gathered[:, 0]
    last_hidden = small_gathered[:, 1].astype(jnp.float32)
    every_flat = small_gathered[:, 2:].reshape(n_seq, -1).astype(jnp.float32)
    mixed_count = decode_mixed.size
    part_max = every_flat[:, :stat_count].reshape((n_seq,) + decode_sum.shape)
    part_sum = (
        every_flat[:, stat_count : 2 * stat_count] + every_flat[:, 2 * stat_count : 3 * stat_count]
    ).reshape((n_seq,) + decode_sum.shape)
    mixed_at = 3 * stat_count
    part_mixed = (
        every_flat[:, mixed_at : mixed_at + mixed_count]
        + every_flat[:, mixed_at + mixed_count : mixed_at + 2 * mixed_count]
    ).reshape((n_seq,) + decode_mixed.shape)

    best = jnp.max(part_max, axis=0)
    factors = jnp.exp(part_max - best[None])
    totals = jnp.sum(part_sum * factors, axis=0)
    mixtures = jnp.sum(part_mixed * factors[..., None], axis=0)
    own_keys = decode_kv[0].reshape(decode_count, kv_local, HEAD_SIZE)
    own_values = decode_kv[1].reshape(decode_count, kv_local, HEAD_SIZE).astype(jnp.float32)
    own_scores = (
        jnp.einsum("bkgh,bkh->bkg", decode_token_rows, own_keys, preferred_element_type=jnp.float32)
        * score_scale
    )
    final_max = jnp.maximum(best, own_scores)
    factor_one = jnp.exp(best - final_max)
    factor_two = jnp.exp(own_scores - final_max)
    final_sum = totals * factor_one + factor_two
    final_mixed = mixtures * factor_one[..., None] + own_values[:, :, None, :] * factor_two[..., None]
    decode_attention = (
        (final_mixed / final_sum[..., None]).astype(jnp.bfloat16).reshape(decode_count, -1)
    )

    blocks_per_tp = n_seq // n_tp
    owner_tp = seq_index // blocks_per_tp
    column_start = (seq_index % blocks_per_tp) * column_width
    decode_hidden_cols = lax.dynamic_slice_in_dim(
        decode_hidden, column_start, column_width, axis=1
    ).astype(jnp.float32)
    last_hidden_cols = lax.dynamic_slice_in_dim(last_hidden, column_start, column_width, axis=1)
    head_hidden_cols = jnp.concatenate([decode_hidden_cols, last_hidden_cols], 0)
    head_attention = jnp.concatenate([decode_attention, last_attention], 0)
    head_part = jnp.dot(head_attention, out_weight, preferred_element_type=jnp.float32)
    head_part = jnp.where(owner_tp == tp_index, head_part + head_hidden_cols, head_part)
    head_all = lax.all_gather(head_part, ("seq", "tp"), axis=0)
    head_rows_count = decode_count + n_seq
    head_all = head_all.reshape(n_seq, n_tp, head_rows_count, column_width)
    head_sum = jnp.sum(head_all, axis=1)
    head_sum = jnp.transpose(head_sum, (1, 0, 2)).reshape(head_rows_count, model_width)
    head_updated = head_sum.astype(jnp.bfloat16)
    decode_out = lax.dynamic_slice_in_dim(
        head_updated[:decode_count], tp_index * feature_width, feature_width, axis=1
    )

    head_input = head_updated.astype(jnp.float32)
    mean_square = jnp.mean(head_input * head_input, axis=-1, keepdims=True)
    normed = (
        head_input * lax.rsqrt(mean_square + norm_eps) * final_gain.astype(jnp.float32)
    ).astype(jnp.bfloat16)
    logits = jnp.dot(normed, head_weight, preferred_element_type=jnp.float32)
    local_max = jnp.max(logits, axis=-1)
    local_sum = jnp.sum(jnp.exp(logits - local_max[:, None]), axis=-1)
    local_stats = jnp.stack([local_max, local_sum], -1)
    every_chunk[1], local_stats = lax.optimization_barrier((every_chunk[1], local_stats))
    stats = doubling_gather(doubling_gather(local_stats, "tp"), "seq").reshape(
        (n_seq * n_tp,) + local_stats.shape
    )
    global_max = jnp.max(stats[..., 0], axis=0)
    global_sum = jnp.sum(stats[..., 1] * jnp.exp(stats[..., 0] - global_max[None]), axis=0)
    log_probs = logits - (global_max + jnp.log(global_sum))[:, None]

    pieces = []
    for rows in every_chunk:
        block = jnp.dot(
            rows.reshape(n_seq * chunk_rows, feature_width),
            out_weight,
            preferred_element_type=jnp.float32,
        ).reshape(n_seq, chunk_rows, column_width)
        if n_tp == 2:
            half = chunk_rows // 2
            mine = lax.dynamic_slice_in_dim(block, tp_index * half, half, axis=1)
            theirs = lax.dynamic_slice_in_dim(block, (1 - tp_index) * half, half, axis=1)
            summed = mine + lax.ppermute(theirs, "tp", [(0, 1), (1, 0)])
        else:
            summed = lax.psum_scatter(block, "tp", scatter_dimension=1, tiled=True)
        by_source = lax.all_to_all(summed, "seq", split_axis=0, concat_axis=0, tiled=True)
        pieces.append(lax.all_to_all(by_source, "tp", split_axis=0, concat_axis=1, tiled=True))
    own_columns = jnp.concatenate(pieces, 1)
    projected = jnp.transpose(own_columns, (1, 0, 2)).reshape(span_len, feature_width)
    prefill_out = (prefill_hidden.astype(jnp.float32) + projected).astype(jnp.bfloat16)


    return (prefill_out, decode_out, log_probs)


def solution(mesh):
    return jax.shard_map(
        local,
        mesh=mesh,
        in_specs=(
            P("seq", "tp"),
            P("seq", "tp"),
            P(None, "seq", "tp"),
            P(None, "seq", None, "tp"),
            P(),
            P(None, "tp"),
            P(None, "tp"),
            P(None, None, "tp"),
            P(None, None, "seq", "tp"),
            P(),
            P(),
            P("tp", "seq"),
            P(),
            P(None, ("seq", "tp")),
        ),
        out_specs=(P("seq", "tp"), P(None, "tp"), P(None, ("seq", "tp"))),
        check_vma=False,
    )
```

```python
import math

import jax
import jax.numpy as jnp
from jax import lax
from jax.sharding import PartitionSpec as P

QUERY_HEADS = 40
KEY_HEADS = 8
HEAD_SIZE = 128


neg_large = -1e30
exact = lax.Precision.HIGHEST
norm_eps = 1e-06


def doubling_gather(value, axis, high_first=False):
    count = lax.axis_size(axis)
    if count & (count - 1):
        return lax.all_gather(value, axis, axis=0)
    index = lax.axis_index(axis)
    block = value[None]
    distances = []
    distance = 1
    while distance < count:
        distances.append(distance)
        distance *= 2
    if high_first:
        distances = distances[::-1]
    for distance in distances:
        pairs = [(i, i ^ distance) for i in range(count)]
        other = lax.ppermute(block, axis, pairs)
        low = (index & distance) == 0
        block = jnp.where(
            low, jnp.concatenate([block, other], 0), jnp.concatenate([other, block], 0)
        )
    if not high_first:
        return block
    steps = len(distances)
    rest = value.shape
    block = block.reshape((2,) * steps + rest)
    order = tuple(range(steps - 1, -1, -1)) + tuple(range(steps, steps + len(rest)))
    return jnp.transpose(block, order).reshape((count,) + rest)


def local(
    prefill_hidden,
    prefill_query_rows,
    prefill_key_value,
    request_prefix_cache,
    prefix_lengths,
    decode_hidden,
    decode_query_rows,
    decode_kv,
    decode_slot_cache,
    cache_lengths,
    slot_table,
    out_weight,
    final_gain,
    head_weight,
):
    query_group_width = QUERY_HEADS // KEY_HEADS
    score_scale = 1.0 / math.sqrt(HEAD_SIZE)
    kv_local = prefill_key_value.shape[2] // HEAD_SIZE
    seq_index = lax.axis_index("seq")
    tp_index = lax.axis_index("tp")
    n_seq = lax.axis_size("seq")
    n_tp = lax.axis_size("tp")
    span_len = prefill_query_rows.shape[0]
    prefix_len = request_prefix_cache.shape[2]
    feature_width = prefill_hidden.shape[1]
    model_width = feature_width * n_tp
    column_width = out_weight.shape[1]
    decode_count = decode_query_rows.shape[0]

    ctx_local = decode_slot_cache.shape[2]
    chosen = jnp.take(decode_slot_cache, slot_table, axis=1)
    positions = seq_index * ctx_local + jnp.arange(ctx_local)
    decode_live = (positions[None, :] < cache_lengths[:, None])[:, None, None, :]
    decode_token_rows = decode_query_rows.reshape(
        decode_count, kv_local, query_group_width, HEAD_SIZE
    )
    cache_keys = chosen[0].reshape(decode_count, ctx_local, kv_local, HEAD_SIZE)
    cache_values = chosen[1].reshape(decode_count, ctx_local, kv_local, HEAD_SIZE)
    decode_scores = (
        jnp.einsum(
            "bkgh,bskh->bkgs", decode_token_rows, cache_keys, preferred_element_type=jnp.float32
        )
        * score_scale
    )
    decode_masked = jnp.where(decode_live, decode_scores, neg_large)
    decode_max = jnp.max(decode_masked, axis=-1).astype(jnp.bfloat16).astype(jnp.float32)
    decode_weights = jnp.where(decode_live, jnp.exp(decode_masked - decode_max[..., None]), 0.0)
    decode_sum = jnp.sum(decode_weights, axis=-1)
    decode_mixed = jnp.einsum(
        "bkgs,bskh->bkgh", decode_weights, cache_values.astype(jnp.float32), precision=exact
    )
    prefix_end = lax.dynamic_slice_in_dim(prefix_lengths, seq_index, 1)[0]
    query_matrix = prefill_query_rows.reshape(span_len, kv_local, query_group_width, HEAD_SIZE)
    joined_keys = jnp.concatenate([request_prefix_cache[0, 0], prefill_key_value[0]], 0).reshape(
        prefix_len + span_len, kv_local, HEAD_SIZE
    )
    value_matrix = jnp.concatenate([request_prefix_cache[1, 0], prefill_key_value[1]], 0).reshape(
        prefix_len + span_len, kv_local, HEAD_SIZE
    )
    key_place = jnp.arange(prefix_len + span_len)
    query_place = jnp.arange(span_len)
    live_mask = jnp.where(
        key_place[None, :] < prefix_len,
        key_place[None, :] < prefix_end,
        key_place[None, :] - prefix_len <= query_place[:, None],
    )
    scores = (
        jnp.einsum("rkgh,skh->kgrs", query_matrix, joined_keys, preferred_element_type=jnp.float32)
        * score_scale
    )
    masked = jnp.where(live_mask, scores, neg_large)
    row_max = jnp.max(masked, axis=-1, keepdims=True)
    weights = jnp.where(live_mask, jnp.exp(masked - row_max), 0.0)
    row_sum = jnp.sum(weights, axis=-1)
    weights_low = weights.astype(jnp.bfloat16)
    mixed = jnp.einsum(
        "kgrs,skh->rkgh", weights_low, value_matrix, preferred_element_type=jnp.float32
    )
    prefill_attention = (
        (mixed / jnp.transpose(row_sum, (2, 0, 1))[..., None])
        .astype(jnp.bfloat16)
        .reshape(span_len, -1)
    )
    sum_high = decode_sum.astype(jnp.bfloat16)
    sum_low = (decode_sum - sum_high.astype(jnp.float32)).astype(jnp.bfloat16)
    mixed_high = decode_mixed.astype(jnp.bfloat16)
    mixed_low = (decode_mixed - mixed_high.astype(jnp.float32)).astype(jnp.bfloat16)
    stat_count = decode_sum.size
    decode_flat = jnp.concatenate(
        [
            decode_max.astype(jnp.bfloat16).reshape(-1),
            sum_high.reshape(-1),
            sum_low.reshape(-1),
            mixed_high.reshape(-1),
            mixed_low.reshape(-1),
        ]
    )
    extra_rows = -(-decode_flat.size // feature_width)
    decode_flat = jnp.pad(decode_flat, (0, extra_rows * feature_width - decode_flat.size))
    small_rows = jnp.concatenate(
        [
            prefill_attention[span_len - 1 :],
            prefill_hidden[span_len - 1 :],
            decode_flat.reshape(extra_rows, feature_width),
        ],
        0,
    )
    small_gathered = doubling_gather(small_rows, "seq", high_first=True)
    every_row = lax.all_gather(prefill_attention, "seq", axis=0).reshape(n_seq * span_len, feature_width)
    last_attention = small_gathered[:, 0]
    last_hidden = small_gathered[:, 1].astype(jnp.float32)
    every_flat = small_gathered[:, 2:].reshape(n_seq, -1).astype(jnp.float32)
    mixed_count = decode_mixed.size
    part_max = every_flat[:, :stat_count].reshape((n_seq,) + decode_sum.shape)
    part_sum = (
        every_flat[:, stat_count : 2 * stat_count] + every_flat[:, 2 * stat_count : 3 * stat_count]
    ).reshape((n_seq,) + decode_sum.shape)
    mixed_at = 3 * stat_count
    part_mixed = (
        every_flat[:, mixed_at : mixed_at + mixed_count]
        + every_flat[:, mixed_at + mixed_count : mixed_at + 2 * mixed_count]
    ).reshape((n_seq,) + decode_mixed.shape)

    best = jnp.max(part_max, axis=0)
    factors = jnp.exp(part_max - best[None])
    totals = jnp.sum(part_sum * factors, axis=0)
    mixtures = jnp.sum(part_mixed * factors[..., None], axis=0)
    own_keys = decode_kv[0].reshape(decode_count, kv_local, HEAD_SIZE)
    own_values = decode_kv[1].reshape(decode_count, kv_local, HEAD_SIZE).astype(jnp.float32)
    own_scores = (
        jnp.einsum("bkgh,bkh->bkg", decode_token_rows, own_keys, preferred_element_type=jnp.float32)
        * score_scale
    )
    final_max = jnp.maximum(best, own_scores)
    factor_one = jnp.exp(best - final_max)
    factor_two = jnp.exp(own_scores - final_max)
    final_sum = totals * factor_one + factor_two
    final_mixed = mixtures * factor_one[..., None] + own_values[:, :, None, :] * factor_two[..., None]
    decode_attention = (
        (final_mixed / final_sum[..., None]).astype(jnp.bfloat16).reshape(decode_count, -1)
    )

    blocks_per_tp = n_seq // n_tp
    owner_tp = seq_index // blocks_per_tp
    column_start = (seq_index % blocks_per_tp) * column_width
    decode_hidden_cols = lax.dynamic_slice_in_dim(
        decode_hidden, column_start, column_width, axis=1
    ).astype(jnp.float32)
    last_hidden_cols = lax.dynamic_slice_in_dim(last_hidden, column_start, column_width, axis=1)
    head_hidden_cols = jnp.concatenate([decode_hidden_cols, last_hidden_cols], 0)
    head_attention = jnp.concatenate([decode_attention, last_attention], 0)
    head_part = jnp.dot(head_attention, out_weight, preferred_element_type=jnp.float32)
    head_part = jnp.where(owner_tp == tp_index, head_part + head_hidden_cols, head_part)
    head_all = lax.all_gather(head_part, ("seq", "tp"), axis=0)
    head_rows_count = decode_count + n_seq
    head_all = head_all.reshape(n_seq, n_tp, head_rows_count, column_width)
    head_sum = jnp.sum(head_all, axis=1)
    head_sum = jnp.transpose(head_sum, (1, 0, 2)).reshape(head_rows_count, model_width)
    head_updated = head_sum.astype(jnp.bfloat16)
    decode_out = lax.dynamic_slice_in_dim(
        head_updated[:decode_count], tp_index * feature_width, feature_width, axis=1
    )

    head_input = head_updated.astype(jnp.float32)
    mean_square = jnp.mean(head_input * head_input, axis=-1, keepdims=True)
    normed = (
        head_input * lax.rsqrt(mean_square + norm_eps) * final_gain.astype(jnp.float32)
    ).astype(jnp.bfloat16)
    logits = jnp.dot(normed, head_weight, preferred_element_type=jnp.float32)
    local_max = jnp.max(logits, axis=-1)
    local_sum = jnp.sum(jnp.exp(logits - local_max[:, None]), axis=-1)
    local_stats = jnp.stack([local_max, local_sum], -1)
    every_row, local_stats = lax.optimization_barrier((every_row, local_stats))
    stats = doubling_gather(doubling_gather(local_stats, "tp"), "seq").reshape(
        (n_seq * n_tp,) + local_stats.shape
    )
    global_max = jnp.max(stats[..., 0], axis=0)
    global_sum = jnp.sum(stats[..., 1] * jnp.exp(stats[..., 0] - global_max[None]), axis=0)
    log_probs = logits - (global_max + jnp.log(global_sum))[:, None]

    column_block = jnp.dot(every_row, out_weight, preferred_element_type=jnp.float32)
    prefill_block = column_block.reshape(n_seq, span_len, column_width)

    summed_rows = lax.psum_scatter(prefill_block, "tp", scatter_dimension=1, tiled=True)
    by_source = lax.all_to_all(
        summed_rows.astype(jnp.bfloat16), "seq", split_axis=0, concat_axis=0, tiled=True
    )
    own_columns = lax.all_to_all(by_source, "tp", split_axis=0, concat_axis=1, tiled=True)
    projected = jnp.transpose(own_columns, (1, 0, 2)).reshape(span_len, feature_width)
    prefill_out = (prefill_hidden.astype(jnp.float32) + projected.astype(jnp.float32)).astype(
        jnp.bfloat16
    )


    return (prefill_out, decode_out, log_probs)


def solution(mesh):
    return jax.shard_map(
        local,
        mesh=mesh,
        in_specs=(
            P("seq", "tp"),
            P("seq", "tp"),
            P(None, "seq", "tp"),
            P(None, "seq", None, "tp"),
            P(),
            P(None, "tp"),
            P(None, "tp"),
            P(None, None, "tp"),
            P(None, None, "seq", "tp"),
            P(),
            P(),
            P("tp", "seq"),
            P(),
            P(None, ("seq", "tp")),
        ),
        out_specs=(P("seq", "tp"), P(None, "tp"), P(None, ("seq", "tp"))),
        check_vma=False,
    )
```

```python
import math

import jax
import jax.numpy as jnp
from jax import lax
from jax.sharding import PartitionSpec as P

QUERY_HEADS = 40
KEY_HEADS = 8
HEAD_SIZE = 128


neg_large = -1e30
exact = lax.Precision.HIGHEST
norm_eps = 1e-06


def doubling_gather(value, axis, high_first=False):
    count = lax.axis_size(axis)
    if count & (count - 1):
        return lax.all_gather(value, axis, axis=0)
    index = lax.axis_index(axis)
    block = value[None]
    distances = []
    distance = 1
    while distance < count:
        distances.append(distance)
        distance *= 2
    if high_first:
        distances = distances[::-1]
    for distance in distances:
        pairs = [(i, i ^ distance) for i in range(count)]
        other = lax.ppermute(block, axis, pairs)
        low = (index & distance) == 0
        block = jnp.where(
            low, jnp.concatenate([block, other], 0), jnp.concatenate([other, block], 0)
        )
    if not high_first:
        return block
    steps = len(distances)
    rest = value.shape
    block = block.reshape((2,) * steps + rest)
    order = tuple(range(steps - 1, -1, -1)) + tuple(range(steps, steps + len(rest)))
    return jnp.transpose(block, order).reshape((count,) + rest)


def local(
    prefill_hidden,
    prefill_query_rows,
    prefill_key_value,
    request_prefix_cache,
    prefix_lengths,
    decode_hidden,
    decode_query_rows,
    decode_kv,
    decode_slot_cache,
    cache_lengths,
    slot_table,
    out_weight,
    final_gain,
    head_weight,
):
    query_group_width = QUERY_HEADS // KEY_HEADS
    score_scale = 1.0 / math.sqrt(HEAD_SIZE)
    kv_local = prefill_key_value.shape[2] // HEAD_SIZE
    seq_index = lax.axis_index("seq")
    tp_index = lax.axis_index("tp")
    n_seq = lax.axis_size("seq")
    n_tp = lax.axis_size("tp")
    span_len = prefill_query_rows.shape[0]
    prefix_len = request_prefix_cache.shape[2]
    feature_width = prefill_hidden.shape[1]
    model_width = feature_width * n_tp
    column_width = out_weight.shape[1]
    decode_count = decode_query_rows.shape[0]

    ctx_local = decode_slot_cache.shape[2]
    chosen = jnp.take(decode_slot_cache, slot_table, axis=1)
    positions = seq_index * ctx_local + jnp.arange(ctx_local)
    decode_live = (positions[None, :] < cache_lengths[:, None])[:, None, None, :]
    decode_token_rows = decode_query_rows.reshape(
        decode_count, kv_local, query_group_width, HEAD_SIZE
    )
    cache_keys = chosen[0].reshape(decode_count, ctx_local, kv_local, HEAD_SIZE)
    cache_values = chosen[1].reshape(decode_count, ctx_local, kv_local, HEAD_SIZE)
    decode_scores = (
        jnp.einsum(
            "bkgh,bskh->bkgs", decode_token_rows, cache_keys, preferred_element_type=jnp.float32
        )
        * score_scale
    )
    decode_masked = jnp.where(decode_live, decode_scores, neg_large)
    decode_max = jnp.max(decode_masked, axis=-1).astype(jnp.bfloat16).astype(jnp.float32)
    decode_weights = jnp.where(decode_live, jnp.exp(decode_masked - decode_max[..., None]), 0.0)
    decode_sum = jnp.sum(decode_weights, axis=-1)
    decode_mixed = jnp.einsum(
        "bkgs,bskh->bkgh", decode_weights, cache_values.astype(jnp.float32), precision=exact
    )
    prefix_end = lax.dynamic_slice_in_dim(prefix_lengths, seq_index, 1)[0]
    query_matrix = prefill_query_rows.reshape(span_len, kv_local, query_group_width, HEAD_SIZE)
    joined_keys = jnp.concatenate([request_prefix_cache[0, 0], prefill_key_value[0]], 0).reshape(
        prefix_len + span_len, kv_local, HEAD_SIZE
    )
    value_matrix = jnp.concatenate([request_prefix_cache[1, 0], prefill_key_value[1]], 0).reshape(
        prefix_len + span_len, kv_local, HEAD_SIZE
    )
    key_place = jnp.arange(prefix_len + span_len)
    query_place = jnp.arange(span_len)
    live_mask = jnp.where(
        key_place[None, :] < prefix_len,
        key_place[None, :] < prefix_end,
        key_place[None, :] - prefix_len <= query_place[:, None],
    )
    scores = (
        jnp.einsum("rkgh,skh->kgrs", query_matrix, joined_keys, preferred_element_type=jnp.float32)
        * score_scale
    )
    masked = jnp.where(live_mask, scores, neg_large)
    row_max = jnp.max(masked, axis=-1, keepdims=True)
    weights = jnp.where(live_mask, jnp.exp(masked - row_max), 0.0)
    row_sum = jnp.sum(weights, axis=-1)
    weights_low = weights.astype(jnp.bfloat16)
    mixed = jnp.einsum(
        "kgrs,skh->rkgh", weights_low, value_matrix, preferred_element_type=jnp.float32
    )
    prefill_attention = (
        (mixed / jnp.transpose(row_sum, (2, 0, 1))[..., None])
        .astype(jnp.bfloat16)
        .reshape(span_len, -1)
    )
    sum_high = decode_sum.astype(jnp.bfloat16)
    sum_low = (decode_sum - sum_high.astype(jnp.float32)).astype(jnp.bfloat16)
    mixed_high = decode_mixed.astype(jnp.bfloat16)
    stat_count = decode_sum.size
    decode_flat = jnp.concatenate(
        [
            decode_max.astype(jnp.bfloat16).reshape(-1),
            sum_high.reshape(-1),
            sum_low.reshape(-1),
            mixed_high.reshape(-1),
        ]
    )
    extra_rows = -(-decode_flat.size // feature_width)
    decode_flat = jnp.pad(decode_flat, (0, extra_rows * feature_width - decode_flat.size))
    small_rows = jnp.concatenate(
        [
            prefill_attention[span_len - 1 :],
            prefill_hidden[span_len - 1 :],
            decode_flat.reshape(extra_rows, feature_width),
        ],
        0,
    )
    small_gathered = doubling_gather(small_rows, "seq", high_first=True)
    every_row = lax.all_gather(prefill_attention, "seq", axis=0).reshape(n_seq * span_len, feature_width)
    last_attention = small_gathered[:, 0]
    last_hidden = small_gathered[:, 1].astype(jnp.float32)
    every_flat = small_gathered[:, 2:].reshape(n_seq, -1).astype(jnp.float32)
    mixed_count = decode_mixed.size
    part_max = every_flat[:, :stat_count].reshape((n_seq,) + decode_sum.shape)
    part_sum = (
        every_flat[:, stat_count : 2 * stat_count] + every_flat[:, 2 * stat_count : 3 * stat_count]
    ).reshape((n_seq,) + decode_sum.shape)
    mixed_at = 3 * stat_count
    part_mixed = (
        every_flat[:, mixed_at : mixed_at + mixed_count]
    ).reshape((n_seq,) + decode_mixed.shape)

    best = jnp.max(part_max, axis=0)
    factors = jnp.exp(part_max - best[None])
    totals = jnp.sum(part_sum * factors, axis=0)
    mixtures = jnp.sum(part_mixed * factors[..., None], axis=0)
    own_keys = decode_kv[0].reshape(decode_count, kv_local, HEAD_SIZE)
    own_values = decode_kv[1].reshape(decode_count, kv_local, HEAD_SIZE).astype(jnp.float32)
    own_scores = (
        jnp.einsum("bkgh,bkh->bkg", decode_token_rows, own_keys, preferred_element_type=jnp.float32)
        * score_scale
    )
    final_max = jnp.maximum(best, own_scores)
    factor_one = jnp.exp(best - final_max)
    factor_two = jnp.exp(own_scores - final_max)
    final_sum = totals * factor_one + factor_two
    final_mixed = mixtures * factor_one[..., None] + own_values[:, :, None, :] * factor_two[..., None]
    decode_attention = (
        (final_mixed / final_sum[..., None]).astype(jnp.bfloat16).reshape(decode_count, -1)
    )

    blocks_per_tp = n_seq // n_tp
    owner_tp = seq_index // blocks_per_tp
    column_start = (seq_index % blocks_per_tp) * column_width
    decode_hidden_cols = lax.dynamic_slice_in_dim(
        decode_hidden, column_start, column_width, axis=1
    ).astype(jnp.float32)
    last_hidden_cols = lax.dynamic_slice_in_dim(last_hidden, column_start, column_width, axis=1)
    head_hidden_cols = jnp.concatenate([decode_hidden_cols, last_hidden_cols], 0)
    head_attention = jnp.concatenate([decode_attention, last_attention], 0)
    head_part = jnp.dot(head_attention, out_weight, preferred_element_type=jnp.float32)
    head_part = jnp.where(owner_tp == tp_index, head_part + head_hidden_cols, head_part)
    head_all = lax.all_gather(head_part, ("seq", "tp"), axis=0)
    head_rows_count = decode_count + n_seq
    head_all = head_all.reshape(n_seq, n_tp, head_rows_count, column_width)
    head_sum = jnp.sum(head_all, axis=1)
    head_sum = jnp.transpose(head_sum, (1, 0, 2)).reshape(head_rows_count, model_width)
    head_updated = head_sum.astype(jnp.bfloat16)
    decode_out = lax.dynamic_slice_in_dim(
        head_updated[:decode_count], tp_index * feature_width, feature_width, axis=1
    )

    head_input = head_updated.astype(jnp.float32)
    mean_square = jnp.mean(head_input * head_input, axis=-1, keepdims=True)
    normed = (
        head_input * lax.rsqrt(mean_square + norm_eps) * final_gain.astype(jnp.float32)
    ).astype(jnp.bfloat16)
    logits = jnp.dot(normed, head_weight, preferred_element_type=jnp.float32)
    local_max = jnp.max(logits, axis=-1)
    local_sum = jnp.sum(jnp.exp(logits - local_max[:, None]), axis=-1)
    local_stats = jnp.stack([local_max, local_sum], -1)
    every_row, local_stats = lax.optimization_barrier((every_row, local_stats))
    stats = doubling_gather(doubling_gather(local_stats, "tp"), "seq").reshape(
        (n_seq * n_tp,) + local_stats.shape
    )
    global_max = jnp.max(stats[..., 0], axis=0)
    global_sum = jnp.sum(stats[..., 1] * jnp.exp(stats[..., 0] - global_max[None]), axis=0)
    log_probs = logits - (global_max + jnp.log(global_sum))[:, None]

    column_block = jnp.dot(every_row, out_weight, preferred_element_type=jnp.float32)
    prefill_block = column_block.reshape(n_seq, span_len, column_width)

    summed_rows = lax.psum_scatter(prefill_block, "tp", scatter_dimension=1, tiled=True)
    by_source = lax.all_to_all(
        summed_rows.astype(jnp.bfloat16), "seq", split_axis=0, concat_axis=0, tiled=True
    )
    own_columns = lax.all_to_all(by_source, "tp", split_axis=0, concat_axis=1, tiled=True)
    projected = jnp.transpose(own_columns, (1, 0, 2)).reshape(span_len, feature_width)
    prefill_out = (prefill_hidden.astype(jnp.float32) + projected.astype(jnp.float32)).astype(
        jnp.bfloat16
    )


    return (prefill_out, decode_out, log_probs)


def solution(mesh):
    return jax.shard_map(
        local,
        mesh=mesh,
        in_specs=(
            P("seq", "tp"),
            P("seq", "tp"),
            P(None, "seq", "tp"),
            P(None, "seq", None, "tp"),
            P(),
            P(None, "tp"),
            P(None, "tp"),
            P(None, None, "tp"),
            P(None, None, "seq", "tp"),
            P(),
            P(),
            P("tp", "seq"),
            P(),
            P(None, ("seq", "tp")),
        ),
        out_specs=(P("seq", "tp"), P(None, "tp"), P(None, ("seq", "tp"))),
        check_vma=False,
    )
```
